32 devices in a mesh: grp: 2 (over x), row: 16 (over z, y, core).
Axes of the slice: x: 2, y: 2, z: 4, core: 2. Of those that a mesh axis runs over, the one named last changes fastest.
Arguments:
- mask_logit: float32 [4096, 256], P(('grp', 'row')), parts along dimension 0, may hold values from -8 to 8
- target: int32 [4096, 256], P(('grp', 'row')), parts along dimension 0, may hold values 0 or 1
- pixel_weight: float32 [4096, 256], P(('grp', 'row')), parts along dimension 0, may hold values from 0.5 to 4
- tile_steps: int32 [2, 32, 2], P(None, ('grp', 'row')), parts along dimension 1, may hold values from 1 to 3, as said below
- pupil_spectra: float32 [2, 12, 32, 32], replicated, may hold values from -32 to 32
- kernel_weight: float32 [12], replicated, may hold values from 0.05 to 0.3
Outputs:
- refined_logit: float32 [4096, 256], P(('grp', 'row')), parts along dimension 0
The draws below stay inside these ranges and needn't reach their ends.
There are 2 independent parts, one for each index of `grp`. The reference program is written for one: setup_inputs(seed, part) draws one part's arguments, and reference() takes and returns one part's arrays. A program takes and returns all parts, laid end to end along the dimension named above; an argument that names none is the same for every part. Nothing has to cross between parts.
Inputs may be any that keep to these rules, and one draw needn't show every extreme that they name: `tile_steps`: a region's number of updates in a round.
All inputs are finite; a program needn't handle non-finite values. No bound on the sum of `target` on one device may be relied on, other than what follows from the above.
Results may differ from the reference program's by a relative error of at most 0.0025.
Values sent between devices are 32-bit elements; how exact they have to be, the bound alone decides.
No kernel may reach another device: no remote copies, remote signals or barrier semaphores. Data moves between devices by JAX's collectives and lax.ppermute only.
A program may use at most 64 MiB of HBM per device.

```python
import math
import jax
import jax.numpy as jnp
from jax import lax

CORE = 128
MARGIN = 128
KF = 32
NK = 12
ROUNDS = 2
TILE = 384
NR = 16
NC = 2
HEIGHT = 2048
WIDTH = 256


def draw_tile_steps(key, part):
    key_busy, key_heavy, key_light, key_first, key_second = jax.random.split(jax.random.fold_in(key, 11), 5)
    busy_rows = jax.random.randint(key_busy, (ROUNDS, NR, 1), 0, 3) == 0
    heavy_counts = jax.random.randint(key_heavy, (ROUNDS, NR, NC), 2, 4)
    light_counts = jax.random.randint(key_light, (ROUNDS, NR, NC), 1, 2)
    flat_counts = jnp.where(busy_rows, heavy_counts, light_counts).reshape(-1)
    total_tiles = ROUNDS * NR * NC
    first_slot = jax.random.randint(key_first, (), 0, total_tiles)
    second_slot = (first_slot + 1 + jax.random.randint(key_second, (), 0, total_tiles - 1)) % total_tiles
    flat_counts = flat_counts.at[first_slot].set(3).at[second_slot].set(1)
    return flat_counts.reshape(ROUNDS, NR, NC).astype(jnp.int32)


def draw_pupil_spectra(key, part):
    dims_all = (2, NK, KF, KF)
    sub_key = jax.random.fold_in(key, 23)
    raw_values = jnp.clip(jax.random.normal(sub_key, dims_all, jnp.float32), -4.0, 4.0)
    positions = jnp.arange(KF)
    centre = (positions[:, None] == KF // 2) & (positions[None, :] == KF // 2)
    return (raw_values * jnp.where(centre, 1.0, 8.0)).astype(jnp.float32)


def set_ends(drawn, stream_key, low, high):
    longest = drawn.shape.index(max(drawn.shape))
    spots = []
    for shift in (0, 1):
        where = [jax.random.randint(jax.random.fold_in(stream_key, axis), (), 0, length) for axis, length in enumerate(drawn.shape)]
        where[longest] = (where[longest] + shift) % drawn.shape[longest]
        spots.append(tuple(where))
    return drawn.at[spots[0]].set(low).at[spots[1]].set(high)


def level_of(own_key, extent, pieces, smallest, high):
    level, own = 1.0, jax.random.fold_in(own_key, 6)
    for position, shards_of in pieces:
        draws = jnp.exp(jax.random.uniform(jax.random.fold_in(own, position), (shards_of,), jnp.float32, smallest / len(pieces), high / len(pieces)))
        level = level * jnp.repeat(draws, extent[position] // shards_of).reshape([-1 if axis == position else 1 for axis in range(len(extent))])
    return level


def normal_values(rng, dims, deviation, reach, pieces=(), kind=jnp.bfloat16):
    entries = deviation * jax.random.normal(rng, dims, jnp.float32)
    if pieces:
        entries = entries * level_of(rng, dims, pieces, -0.22, 0.18)
    return jnp.clip(entries, -reach, reach).astype(kind)


def setup_inputs(seed: int = 0, part: int = 0) -> dict:
    key_list = jax.random.split(jax.random.key(seed), 7)
    part_keys = jax.random.split(jax.random.fold_in(key_list[6], part), 7)
    return {
        "mask_logit": normal_values(part_keys[0], (HEIGHT, WIDTH), 1.5, 8.0, ((0, 16),), jnp.float32),
        "target": set_ends((jax.random.randint(part_keys[1], (HEIGHT, WIDTH), 0, 2) < 1).astype(jnp.int32), jax.random.fold_in(part_keys[1], 1), 0, 1),
        "pixel_weight": jnp.clip(jnp.exp(math.log(4.0) - 2.0794415 * jax.random.uniform(part_keys[2], (HEIGHT, WIDTH), jnp.float32) ** level_of(part_keys[2], (HEIGHT, WIDTH), ((0, 16),), -0.2, 0.2)), 0.5, 4.0),
        "tile_steps": draw_tile_steps(jax.random.fold_in(jax.random.fold_in(key_list[6], part), 71), part),
        "pupil_spectra": draw_pupil_spectra(jax.random.fold_in(key_list[6], 71), part),
        "kernel_weight": jnp.clip(jnp.exp(jax.random.uniform(key_list[5], (NK,), jnp.float32, math.log(0.05), math.log(0.3))), 0.05, 0.3),
    }


resist_slope = 4.0
resist_level = 1.0
step_rate = 0.1

def spectral_tables(side_len, freq_count):
    freq_values = jnp.arange(freq_count, dtype=jnp.int32) - freq_count // 2
    pixel_pos = jnp.arange(side_len, dtype=jnp.int32)
    phase_idx = jnp.mod(freq_values[:, None] * pixel_pos[None, :], side_len)
    angles = phase_idx.astype(jnp.float32) * (2.0 * math.pi / side_len)
    return (jnp.cos(angles), jnp.sin(angles))

def descend(tile_logit, tile_comb, tile_count, cosine_table, sine_table, pupil_spectra, kernel_weight):
    freq_count = cosine_table.shape[0]
    side_len = cosine_table.shape[1]
    kernels = pupil_spectra.shape[1]
    highest = lax.Precision.HIGHEST
    basis_full = jnp.concatenate([cosine_table, sine_table], axis=0)
    basis_bf = basis_full.astype(jnp.bfloat16)
    target_on = (tile_comb > 0).astype(jnp.float32)
    weight_abs = jnp.abs(tile_comb)
    weight_cols = kernel_weight[None, :, None, None]
    norm_area = float(side_len * side_len)
    pupil_re = pupil_spectra[0]
    pupil_im = pupil_spectra[1]
    contract_first = (((0,), (0,)), ((), ()))

    def one_update(logit_now):
        mask_soft = jax.nn.sigmoid(logit_now)
        mask_bf = mask_soft.astype(jnp.bfloat16)
        upper_rows = jnp.dot(basis_bf, mask_bf, preferred_element_type=jnp.float32)
        cross_mat = jnp.dot(upper_rows, basis_full.T, precision=highest) / norm_area
        spec_re = cross_mat[:freq_count, :freq_count] - cross_mat[freq_count:, freq_count:]
        spec_im = -(cross_mat[:freq_count, freq_count:] + cross_mat[freq_count:, :freq_count])
        amp_re = pupil_re * spec_re - pupil_im * spec_im
        amp_im = pupil_re * spec_im + pupil_im * spec_re
        wave_re = jnp.einsum('kfg,gy->kfy', amp_re, cosine_table, precision=highest) - jnp.einsum('kfg,gy->kfy', amp_im, sine_table, precision=highest)
        wave_im = jnp.einsum('kfg,gy->kfy', amp_re, sine_table, precision=highest) + jnp.einsum('kfg,gy->kfy', amp_im, cosine_table, precision=highest)
        wave_top = jnp.stack([wave_re, wave_im], axis=1)
        wave_low = jnp.stack([-wave_im, wave_re], axis=1)
        wave_block = jnp.concatenate([wave_top, wave_low], axis=2)
        wave_block = jnp.transpose(wave_block, (2, 0, 1, 3)).reshape(2 * freq_count, kernels * 2 * side_len).astype(jnp.bfloat16)
        field_bf = lax.dot_general(basis_bf, wave_block, contract_first, preferred_element_type=jnp.float32).astype(jnp.bfloat16)
        field_all = field_bf.astype(jnp.float32).reshape(side_len, kernels, 2, side_len)
        intensity = lax.optimization_barrier(jnp.sum(weight_cols * field_all * field_all, axis=(1, 2)))
        resist = jax.nn.sigmoid(resist_slope * (intensity - resist_level))
        error_term = 2.0 * resist_slope * weight_abs * (resist - target_on) * resist * (1.0 - resist)
        grad_bf = (2.0 * weight_cols * error_term[:, None, None, :] * field_all).reshape(side_len, kernels * 2 * side_len).astype(jnp.bfloat16)
        back_proj = jnp.dot(basis_bf, grad_bf, preferred_element_type=jnp.float32).reshape(2 * freq_count, kernels, 2, side_len)
        dwave_re = back_proj[:freq_count, :, 0] + back_proj[freq_count:, :, 1]
        dwave_im = back_proj[:freq_count, :, 1] - back_proj[freq_count:, :, 0]
        damp_re = jnp.einsum('fky,gy->kfg', dwave_re, cosine_table, precision=highest) + jnp.einsum('fky,gy->kfg', dwave_im, sine_table, precision=highest)
        damp_im = jnp.einsum('fky,gy->kfg', dwave_im, cosine_table, precision=highest) - jnp.einsum('fky,gy->kfg', dwave_re, sine_table, precision=highest)
        dspec_re = lax.optimization_barrier(jnp.sum(pupil_re * damp_re + pupil_im * damp_im, axis=0))
        dspec_im = lax.optimization_barrier(jnp.sum(pupil_re * damp_im - pupil_im * damp_re, axis=0))
        dcross = jnp.concatenate([jnp.concatenate([dspec_re, -dspec_im], axis=1), jnp.concatenate([-dspec_im, -dspec_re], axis=1)], axis=0)
        dupper = jnp.dot(dcross, basis_full, precision=highest) / norm_area
        dmask = lax.dot_general(basis_bf, dupper.astype(jnp.bfloat16), contract_first, preferred_element_type=jnp.float32)
        grad_logit = dmask * mask_soft * (1.0 - mask_soft)
        step_scale = lax.rsqrt(jnp.mean(grad_logit * grad_logit) + 1e-06)
        return logit_now - step_rate * step_scale * grad_logit

    def keep_going(carry):
        return carry[0] < tile_count

    def advance(carry):
        return (carry[0] + 1, one_update(carry[1]))
    final_pair = lax.while_loop(keep_going, advance, (jnp.int32(0), tile_logit))
    return final_pair[1]

def reference(mask_logit, target, pixel_weight, tile_steps, pupil_spectra, kernel_weight):
    cosine_table, sine_table = spectral_tables(TILE, KF)
    combined = jnp.where(target == 1, pixel_weight, -pixel_weight)
    padded_comb = jnp.pad(combined, MARGIN)
    state_field = mask_logit
    for round_index in range(ROUNDS):
        padded_state = jnp.pad(state_field, MARGIN)

        def run_region(region_id):
            row_region = region_id // NC
            col_region = region_id % NC
            row_start = (row_region * CORE).astype(jnp.int32)
            col_start = (col_region * CORE).astype(jnp.int32)
            tile_logit = lax.dynamic_slice(padded_state, (row_start, col_start), (TILE, TILE))
            tile_comb = lax.dynamic_slice(padded_comb, (row_start, col_start), (TILE, TILE))
            tile_count = tile_steps[round_index, row_region, col_region]
            updated = descend(tile_logit, tile_comb, tile_count, cosine_table, sine_table, pupil_spectra, kernel_weight)
            return updated[MARGIN:MARGIN + CORE, MARGIN:MARGIN + CORE]
        region_cores = lax.map(run_region, jnp.arange(NR * NC, dtype=jnp.int32))
        state_field = jnp.transpose(region_cores.reshape(NR, NC, CORE, CORE), (0, 2, 1, 3)).reshape(NR * CORE, NC * CORE)
    return state_field
```

```python
import math

import jax
import jax.numpy as jnp
from jax import lax
from jax.experimental import pallas as pl
from jax.experimental.pallas import tpu as pltpu
from jax.sharding import PartitionSpec as P

CORE = 128
TILES_DEV = 2
MARGIN = 128
KF = 32
ROUNDS = 2
TILE = 384


resist_slope = 4.0
resist_level = 1.0
step_rate = 0.1


def extended_2(shard, sides, width):
    for axis, dim in sides:
        size, length = (lax.axis_size(axis), shard.shape[dim])
        up = [(i, (i + 1) % size) for i in range(size - 1)]
        down = [(j, i) for i, j in up]
        last = lax.slice_in_dim(shard, length - width, length, axis=dim)
        first = lax.slice_in_dim(shard, 0, width, axis=dim)
        before = lax.ppermute(last, axis, up)
        after = lax.ppermute(first, axis, down)
        shard = jnp.concatenate([before, shard, after], axis=dim)
    return shard


def spectral_tables(side_len, freq_count):
    freq_values = jnp.arange(freq_count, dtype=jnp.int32) - freq_count // 2
    pixel_pos = jnp.arange(side_len, dtype=jnp.int32)
    phase_idx = jnp.mod(freq_values[:, None] * pixel_pos[None, :], side_len)
    angles = phase_idx.astype(jnp.float32) * (2.0 * math.pi / side_len)
    return (jnp.cos(angles), jnp.sin(angles))


def descend(
    tile_logit, tile_comb, tile_count, cosine_table, sine_table, pupil_spectra, kernel_weight
):
    freq_count = cosine_table.shape[0]
    side_len = cosine_table.shape[1]
    kernels = pupil_spectra.shape[1]
    highest = lax.Precision.HIGHEST
    basis_full = jnp.concatenate([cosine_table, sine_table], axis=0)
    basis_bf = basis_full.astype(jnp.bfloat16)
    basis_t = basis_bf.T
    target_on = (tile_comb > 0).astype(jnp.float32)
    weight_abs = jnp.abs(tile_comb)
    weight_cols = kernel_weight[None, :, None, None]
    norm_area = float(side_len * side_len)
    pupil_re = pupil_spectra[0]
    pupil_im = pupil_spectra[1]
    contract_first = (((0,), (0,)), ((), ()))

    def one_update(logit_now):
        mask_soft = jax.nn.sigmoid(logit_now)
        mask_bf = mask_soft.astype(jnp.bfloat16)
        upper_rows = jnp.dot(basis_bf, mask_bf, preferred_element_type=jnp.float32)
        cross_mat = jnp.dot(upper_rows, basis_full.T, precision=highest) / norm_area
        spec_re = cross_mat[:freq_count, :freq_count] - cross_mat[freq_count:, freq_count:]
        spec_im = -(cross_mat[:freq_count, freq_count:] + cross_mat[freq_count:, :freq_count])
        amp_re = pupil_re * spec_re - pupil_im * spec_im
        amp_im = pupil_re * spec_im + pupil_im * spec_re
        wave_re = jnp.einsum("kfg,gy->kfy", amp_re, cosine_table, precision=highest) - jnp.einsum(
            "kfg,gy->kfy", amp_im, sine_table, precision=highest
        )
        wave_im = jnp.einsum("kfg,gy->kfy", amp_re, sine_table, precision=highest) + jnp.einsum(
            "kfg,gy->kfy", amp_im, cosine_table, precision=highest
        )
        wave_c0 = jnp.concatenate([wave_re, -wave_im], axis=1)
        wave_c1 = jnp.concatenate([wave_im, wave_re], axis=1)
        wave_block = jnp.stack([wave_c0, wave_c1], axis=1).astype(jnp.bfloat16)
        dwave_re, dwave_im = middle_call(
            kernel_weight, basis_t, basis_bf, wave_block, weight_abs, target_on
        )
        damp_re = jnp.einsum("kfy,gy->kfg", dwave_re, cosine_table, precision=highest) + jnp.einsum(
            "kfy,gy->kfg", dwave_im, sine_table, precision=highest
        )
        damp_im = jnp.einsum("kfy,gy->kfg", dwave_im, cosine_table, precision=highest) - jnp.einsum(
            "kfy,gy->kfg", dwave_re, sine_table, precision=highest
        )
        dspec_re = jnp.sum(pupil_re * damp_re + pupil_im * damp_im, axis=0)
        dspec_im = jnp.sum(pupil_re * damp_im - pupil_im * damp_re, axis=0)
        dcross = jnp.concatenate(
            [
                jnp.concatenate([dspec_re, -dspec_im], axis=1),
                jnp.concatenate([-dspec_im, -dspec_re], axis=1),
            ],
            axis=0,
        )
        dupper = jnp.dot(dcross, basis_full, precision=highest) / norm_area
        dmask = lax.dot_general(
            basis_bf,
            dupper.astype(jnp.bfloat16),
            contract_first,
            preferred_element_type=jnp.float32,
        )
        grad_logit = dmask * mask_soft * (1.0 - mask_soft)
        step_scale = lax.rsqrt(jnp.mean(grad_logit * grad_logit) + 1e-06)
        return logit_now - step_rate * step_scale * grad_logit

    def keep_going(carry):
        return carry[0] < tile_count

    def advance(carry):
        return (carry[0] + 1, one_update(carry[1]))

    final_pair = lax.while_loop(keep_going, advance, (jnp.int32(0), tile_logit))
    return final_pair[1]


def middle_kernel(w_ref, bt_ref, b_ref, wave_ref, wabs_ref, ton_ref, dre_ref, dim_ref, field_scr, inten_scr, err_scr):
    kernels = wave_ref.shape[0]
    half = dre_ref.shape[1]
    inten_scr[...] = jnp.zeros_like(inten_scr)

    def forward(k, carry):
        w = w_ref[k]
        basis_t = bt_ref[...]
        f_re = jnp.dot(basis_t, wave_ref[k, 0], preferred_element_type=jnp.float32).astype(jnp.bfloat16)
        f_im = jnp.dot(basis_t, wave_ref[k, 1], preferred_element_type=jnp.float32).astype(jnp.bfloat16)
        field_scr[k, 0] = f_re
        field_scr[k, 1] = f_im
        a = f_re.astype(jnp.float32)
        b = f_im.astype(jnp.float32)
        inten_scr[...] += w * a * a + w * b * b
        return carry

    lax.fori_loop(0, kernels, forward, 0)
    resist = jax.nn.sigmoid(resist_slope * (inten_scr[...] - resist_level))
    err_scr[...] = 2.0 * resist_slope * wabs_ref[...] * (resist - ton_ref[...]) * resist * (1.0 - resist)

    def backward(k, carry):
        scale = 2.0 * w_ref[k] * err_scr[...]
        basis = b_ref[...]
        g_re = (scale * field_scr[k, 0].astype(jnp.float32)).astype(jnp.bfloat16)
        g_im = (scale * field_scr[k, 1].astype(jnp.float32)).astype(jnp.bfloat16)
        p_re = jnp.dot(basis, g_re, preferred_element_type=jnp.float32)
        p_im = jnp.dot(basis, g_im, preferred_element_type=jnp.float32)
        dre_ref[k] = p_re[:half] + p_im[half:]
        dim_ref[k] = p_im[:half] - p_re[half:]
        return carry

    lax.fori_loop(0, kernels, backward, 0)


def middle_call(kernel_weight, basis_t, basis_bf, wave_block, weight_abs, target_on):
    kernels, _, rows, side = wave_block.shape
    half = rows // 2
    vmem = pltpu.MemorySpace.VMEM
    out = jax.ShapeDtypeStruct((kernels, half, side), jnp.float32)
    return pl.pallas_call(
        middle_kernel,
        out_shape=(out, out),
        in_specs=[pl.BlockSpec(memory_space=pltpu.MemorySpace.SMEM)] + [pl.BlockSpec(memory_space=vmem)] * 5,
        out_specs=(pl.BlockSpec(memory_space=vmem), pl.BlockSpec(memory_space=vmem)),
        scratch_shapes=[
            pltpu.VMEM((kernels, 2, side, side), jnp.bfloat16),
            pltpu.VMEM((side, side), jnp.float32),
            pltpu.VMEM((side, side), jnp.float32),
        ],
        compiler_params=pltpu.CompilerParams(vmem_limit_bytes=48 * 1024 * 1024),
    )(kernel_weight, basis_t, basis_bf, wave_block, weight_abs, target_on)


def on_device(mask_logit, target, pixel_weight, tile_steps, pupil_spectra, kernel_weight):
    cosine_table, sine_table = spectral_tables(TILE, KF)
    combined = jnp.where(target == 1, pixel_weight, -pixel_weight)

    def run_tile(packed):
        tile_logit, tile_comb, tile_count = packed
        updated = descend(
            tile_logit,
            tile_comb,
            tile_count,
            cosine_table,
            sine_table,
            pupil_spectra,
            kernel_weight,
        )
        return updated[MARGIN : MARGIN + CORE, MARGIN : MARGIN + CORE]

    def cut_tiles(extended):
        widened = jnp.pad(extended, ((0, 0), (MARGIN, MARGIN)))
        return jnp.stack(
            [widened[:, column * CORE : column * CORE + TILE] for column in range(TILES_DEV)]
        )

    state_field = mask_logit
    for round_index in range(ROUNDS):
        both_ext = extended_2(jnp.stack([state_field, combined]), (("row", 1),), MARGIN)
        logit_tiles = cut_tiles(both_ext[0])
        comb_tiles = cut_tiles(both_ext[1])
        own_steps = tile_steps[round_index, 0]
        own_cores = lax.map(run_tile, (logit_tiles, comb_tiles, own_steps))
        state_field = jnp.transpose(own_cores, (1, 0, 2)).reshape(CORE, TILES_DEV * CORE)
    return state_field


def solution(mesh):
    return jax.shard_map(
        on_device,
        mesh=mesh,
        in_specs=(
            P(("grp", "row"), None),
            P(("grp", "row"), None),
            P(("grp", "row"), None),
            P(None, ("grp", "row"), None),
            P(),
            P(),
        ),
        out_specs=P(("grp", "row"), None),
        check_vma=False,
    )
```

```python
import math

import jax
import jax.numpy as jnp
from jax import lax
from jax.experimental import pallas as pl
from jax.experimental.pallas import tpu as pltpu
from jax.sharding import PartitionSpec as P

CORE = 128
MARGIN = 128
KF = 32
ROUNDS = 2
TILE = 384


resist_slope = 4.0
resist_level = 1.0
step_rate = 0.1


def extended_2(shard, sides, width):
    for axis, dim in sides:
        size, length = (lax.axis_size(axis), shard.shape[dim])
        up = [(i, (i + 1) % size) for i in range(size - 1)]
        down = [(j, i) for i, j in up]
        last = lax.slice_in_dim(shard, length - width, length, axis=dim)
        first = lax.slice_in_dim(shard, 0, width, axis=dim)
        before = lax.ppermute(last, axis, up)
        after = lax.ppermute(first, axis, down)
        shard = jnp.concatenate([before, shard, after], axis=dim)
    return shard


def spectral_tables(side_len, freq_count):
    freq_values = jnp.arange(freq_count, dtype=jnp.int32) - freq_count // 2
    pixel_pos = jnp.arange(side_len, dtype=jnp.int32)
    phase_idx = jnp.mod(freq_values[:, None] * pixel_pos[None, :], side_len)
    angles = phase_idx.astype(jnp.float32) * (2.0 * math.pi / side_len)
    return (jnp.cos(angles), jnp.sin(angles))


def tile_kernel(
    steps_ref, w_ref, logit_ref, comb_ref, pre_ref, pim_ref, bt_ref, b_ref, ct_ref, st_ref,
    c_ref, s_ref, wcs_ref, wsc_ref, out_ref, logit_scr, wre_scr, wim_scr, field_scr,
    inten_scr, err_scr, dre_scr, dim_scr,
):
    kernels = field_scr.shape[0]
    freq = c_ref.shape[0]
    side = c_ref.shape[1]
    norm_area = float(side * side)
    hp = lax.Precision.HIGHEST
    f32 = jnp.float32
    bf16 = jnp.bfloat16

    def mm(a, b):
        return jnp.dot(a, b, precision=hp, preferred_element_type=f32)

    logit_scr[...] = logit_ref[0]

    def forward(k, carry):
        r0 = pl.multiple_of(k * freq, freq)
        a0 = wre_scr[pl.ds(r0, freq), :]
        a1 = wim_scr[pl.ds(r0, freq), :]
        c0 = jnp.concatenate([a0, -a1], axis=0)
        c1 = jnp.concatenate([a1, a0], axis=0)
        basis_t = bt_ref[...]
        f_re = jnp.dot(basis_t, c0, preferred_element_type=f32).astype(bf16)
        f_im = jnp.dot(basis_t, c1, preferred_element_type=f32).astype(bf16)
        field_scr[k, 0] = f_re
        field_scr[k, 1] = f_im
        w = w_ref[k]
        a = f_re.astype(f32)
        b = f_im.astype(f32)
        inten_scr[...] += w * a * a + w * b * b
        return carry

    def backward(k, carry):
        scale = 2.0 * w_ref[k] * err_scr[...]
        basis = b_ref[...]
        g_re = (scale * field_scr[k, 0].astype(f32)).astype(bf16)
        g_im = (scale * field_scr[k, 1].astype(f32)).astype(bf16)
        p_re = jnp.dot(basis, g_re, preferred_element_type=f32)
        p_im = jnp.dot(basis, g_im, preferred_element_type=f32)
        r0 = pl.multiple_of(k * freq, freq)
        dre_scr[pl.ds(r0, freq), :] = p_re[:freq] + p_im[freq:]
        dim_scr[pl.ds(r0, freq), :] = p_im[:freq] - p_re[freq:]
        return carry

    def update(step, carry):
        logit = logit_scr[...]
        mask_soft = jax.nn.sigmoid(logit)
        upper = jnp.dot(b_ref[...], mask_soft.astype(bf16), preferred_element_type=f32)
        u_top = upper[:freq]
        u_bot = upper[freq:]
        q11 = mm(u_top, ct_ref[...]) / norm_area
        q12 = mm(u_top, st_ref[...]) / norm_area
        q21 = mm(u_bot, ct_ref[...]) / norm_area
        q22 = mm(u_bot, st_ref[...]) / norm_area
        spec_re = q11 - q22
        spec_im = -(q12 + q21)
        sre = jnp.concatenate([spec_re] * kernels, axis=0)
        sim = jnp.concatenate([spec_im] * kernels, axis=0)
        pre = pre_ref[...]
        pim = pim_ref[...]
        amp_re = pre * sre - pim * sim
        amp_im = pre * sim + pim * sre
        waves = mm(amp_re, wcs_ref[...]) + mm(amp_im, wsc_ref[...])
        wre_scr[...] = waves[:, :side].astype(bf16)
        wim_scr[...] = waves[:, side:].astype(bf16)
        inten_scr[...] = jnp.zeros_like(inten_scr)
        lax.fori_loop(0, kernels, forward, 0)
        resist = jax.nn.sigmoid(resist_slope * (inten_scr[...] - resist_level))
        comb = comb_ref[0]
        target_on = (comb > 0).astype(f32)
        weight_abs = jnp.abs(comb)
        err_scr[...] = 2.0 * resist_slope * weight_abs * (resist - target_on) * resist * (1.0 - resist)
        lax.fori_loop(0, kernels, backward, 0)
        dre = dre_scr[...]
        dim = dim_scr[...]
        damp_re = mm(dre, ct_ref[...]) + mm(dim, st_ref[...])
        damp_im = mm(dim, ct_ref[...]) - mm(dre, st_ref[...])
        t_re = pre * damp_re + pim * damp_im
        t_im = pre * damp_im - pim * damp_re
        dspec_re = t_re[:freq]
        dspec_im = t_im[:freq]
        for i in range(1, kernels):
            dspec_re = dspec_re + t_re[i * freq:(i + 1) * freq]
            dspec_im = dspec_im + t_im[i * freq:(i + 1) * freq]
        cos_t = c_ref[...]
        sin_t = s_ref[...]
        top = mm(dspec_re, cos_t) + mm(-dspec_im, sin_t)
        bot = mm(-dspec_im, cos_t) + mm(-dspec_re, sin_t)
        dupper = jnp.concatenate([top, bot], axis=0) / norm_area
        dmask = jnp.dot(bt_ref[...], dupper.astype(bf16), preferred_element_type=f32)
        grad_logit = dmask * mask_soft * (1.0 - mask_soft)
        step_scale = lax.rsqrt(jnp.mean(grad_logit * grad_logit) + 1e-06)
        logit_scr[...] = logit - step_rate * step_scale * grad_logit
        return carry

    lax.fori_loop(0, steps_ref[pl.program_id(0)], update, 0)
    out_ref[0] = logit_scr[MARGIN:MARGIN + CORE, MARGIN:MARGIN + CORE]


def tiles_call(steps, kernel_weight, logit_tiles, comb_tiles, pupil_spectra, cosine_table, sine_table):
    tiles = logit_tiles.shape[0]
    kernels = pupil_spectra.shape[1]
    freq, side = cosine_table.shape
    basis_full = jnp.concatenate([cosine_table, sine_table], axis=0)
    basis_bf = basis_full.astype(jnp.bfloat16)
    pre = pupil_spectra[0].reshape(kernels * freq, freq)
    pim = pupil_spectra[1].reshape(kernels * freq, freq)
    wcs = jnp.concatenate([cosine_table, sine_table], axis=1)
    wsc = jnp.concatenate([-sine_table, cosine_table], axis=1)
    consts = [pre, pim, basis_bf.T, basis_bf, cosine_table.T, sine_table.T, cosine_table, sine_table, wcs, wsc]
    smem = pl.BlockSpec(memory_space=pltpu.MemorySpace.SMEM)
    tile_spec = pl.BlockSpec((1, side, side), lambda t: (t, 0, 0))
    const_specs = [pl.BlockSpec(c.shape, lambda t: (0, 0)) for c in consts]
    return pl.pallas_call(
        tile_kernel,
        grid=(tiles,),
        out_shape=jax.ShapeDtypeStruct((tiles, CORE, CORE), jnp.float32),
        in_specs=[smem, smem, tile_spec, tile_spec] + const_specs,
        out_specs=pl.BlockSpec((1, CORE, CORE), lambda t: (t, 0, 0)),
        scratch_shapes=[
            pltpu.VMEM((side, side), jnp.float32),
            pltpu.VMEM((kernels * freq, side), jnp.bfloat16),
            pltpu.VMEM((kernels * freq, side), jnp.bfloat16),
            pltpu.VMEM((kernels, 2, side, side), jnp.bfloat16),
            pltpu.VMEM((side, side), jnp.float32),
            pltpu.VMEM((side, side), jnp.float32),
            pltpu.VMEM((kernels * freq, side), jnp.float32),
            pltpu.VMEM((kernels * freq, side), jnp.float32),
        ],
        compiler_params=pltpu.CompilerParams(vmem_limit_bytes=48 * 1024 * 1024),
    )(steps, kernel_weight, logit_tiles, comb_tiles, *consts)


def on_device(mask_logit, target, pixel_weight, tile_steps, pupil_spectra, kernel_weight):
    cosine_table, sine_table = spectral_tables(TILE, KF)
    combined = jnp.where(target == 1, pixel_weight, -pixel_weight)
    tiles_dev = mask_logit.shape[1] // CORE

    def cut_tiles(extended):
        widened = jnp.pad(extended, ((0, 0), (MARGIN, MARGIN)))
        return jnp.stack(
            [widened[:, column * CORE : column * CORE + TILE] for column in range(tiles_dev)]
        )

    state_field = mask_logit
    for round_index in range(ROUNDS):
        both_ext = extended_2(jnp.stack([state_field, combined]), (("row", 1),), MARGIN)
        logit_tiles = cut_tiles(both_ext[0])
        comb_tiles = cut_tiles(both_ext[1])
        own_steps = tile_steps[round_index, 0]
        own_cores = tiles_call(
            own_steps, kernel_weight, logit_tiles, comb_tiles, pupil_spectra, cosine_table, sine_table
        )
        state_field = jnp.transpose(own_cores, (1, 0, 2)).reshape(CORE, tiles_dev * CORE)
    return state_field


def solution(mesh):
    return jax.shard_map(
        on_device,
        mesh=mesh,
        in_specs=(
            P(("grp", "row"), None),
            P(("grp", "row"), None),
            P(("grp", "row"), None),
            P(None, ("grp", "row"), None),
            P(),
            P(),
        ),
        out_specs=P(("grp", "row"), None),
        check_vma=False,
    )
```

```python
import math

import jax
import jax.numpy as jnp
from jax import lax
from jax.experimental import pallas as pl
from jax.experimental.pallas import tpu as pltpu
from jax.sharding import PartitionSpec as P

CORE = 128
MARGIN = 128
KF = 32
ROUNDS = 2
TILE = 384


resist_slope = 4.0
resist_level = 1.0
step_rate = 0.1


def extended_2(shard, sides, width):
    for axis, dim in sides:
        size, length = (lax.axis_size(axis), shard.shape[dim])
        up = [(i, (i + 1) % size) for i in range(size - 1)]
        down = [(j, i) for i, j in up]
        last = lax.slice_in_dim(shard, length - width, length, axis=dim)
        first = lax.slice_in_dim(shard, 0, width, axis=dim)
        before = lax.ppermute(last, axis, up)
        after = lax.ppermute(first, axis, down)
        shard = jnp.concatenate([before, shard, after], axis=dim)
    return shard


def spectral_tables(side_len, freq_count):
    freq_values = jnp.arange(freq_count, dtype=jnp.int32) - freq_count // 2
    pixel_pos = jnp.arange(side_len, dtype=jnp.int32)
    phase_idx = jnp.mod(freq_values[:, None] * pixel_pos[None, :], side_len)
    angles = phase_idx.astype(jnp.float32) * (2.0 * math.pi / side_len)
    return (jnp.cos(angles), jnp.sin(angles))


def split_bf(x):
    hi = x.astype(jnp.bfloat16)
    lo = (x - hi.astype(jnp.float32)).astype(jnp.bfloat16)
    return hi, lo


def tile_kernel(
    steps_ref, w_ref, logit_ref, comb_ref, pre_ref, pim_ref, bt_ref, b_ref, t1_ref, wv_ref, t2_ref,
    t3_ref, out_ref, logit_scr, t1h, t1l, wvh, wvl, t2h, t2l, t3h, t3l, wre_scr, wim_scr,
    field_scr, inten_scr, err_scr, dcat_scr,
):
    kernels = field_scr.shape[0]
    side = field_scr.shape[2]
    freq = wre_scr.shape[0] // kernels
    lane = pre_ref.shape[1]
    norm_area = float(side * side)
    f32 = jnp.float32
    bf16 = jnp.bfloat16

    def dot(a, b):
        return jnp.dot(a, b, preferred_element_type=f32)

    for table, hi_ref, lo_ref in ((t1_ref, t1h, t1l), (wv_ref, wvh, wvl), (t2_ref, t2h, t2l), (t3_ref, t3h, t3l)):
        hi, lo = split_bf(table[...])
        hi_ref[...] = hi
        lo_ref[...] = lo

    def mm3(x, hi_ref, lo_ref):
        x_hi, x_lo = split_bf(x)
        t_hi = hi_ref[...]
        return dot(x_hi, t_hi) + (dot(x_lo, t_hi) + dot(x_hi, lo_ref[...]))

    logit_scr[...] = logit_ref[0]

    def forward(k, carry):
        r0 = pl.multiple_of(k * freq, freq)
        a0 = wre_scr[pl.ds(r0, freq), :]
        a1 = wim_scr[pl.ds(r0, freq), :]
        c0 = jnp.concatenate([a0, -a1], axis=0)
        c1 = jnp.concatenate([a1, a0], axis=0)
        basis_t = bt_ref[...]
        f_re = dot(basis_t, c0).astype(bf16).astype(f32)
        f_im = dot(basis_t, c1).astype(bf16).astype(f32)
        field_scr[k, 0] = f_re
        field_scr[k, 1] = f_im
        inten_scr[...] += w_ref[k] * (f_re * f_re + f_im * f_im)
        return carry

    def backward(k, carry):
        scale = w_ref[k] * err_scr[...]
        basis = b_ref[...]
        g_re = (scale * field_scr[k, 0]).astype(bf16)
        g_im = (scale * field_scr[k, 1]).astype(bf16)
        p_re = dot(basis, g_re)
        p_im = dot(basis, g_im)
        r0 = pl.multiple_of(k * freq, freq)
        dcat_scr[pl.ds(r0, freq), :side] = p_re[:freq] + p_im[freq:]
        dcat_scr[pl.ds(r0, freq), side:] = p_im[:freq] - p_re[freq:]
        return carry

    def update(step, carry):
        logit = logit_scr[...]
        mask_soft = jax.nn.sigmoid(logit)
        upper = dot(b_ref[...], mask_soft.astype(bf16))
        cross = mm3(upper, t1h, t1l) / norm_area
        spec_re = cross[:freq, :lane] - cross[freq:, lane:]
        spec_im = -(cross[:freq, lane:] + cross[freq:, :lane])
        sre = jnp.concatenate([spec_re] * kernels, axis=0)
        sim = jnp.concatenate([spec_im] * kernels, axis=0)
        pre = pre_ref[...]
        pim = pim_ref[...]
        amp_re = pre * sre - pim * sim
        amp_im = pre * sim + pim * sre
        waves = mm3(jnp.concatenate([amp_re, amp_im], axis=1), wvh, wvl)
        wre_scr[...] = waves[:, :side].astype(bf16)
        wim_scr[...] = waves[:, side:].astype(bf16)
        inten_scr[...] = jnp.zeros_like(inten_scr)
        lax.fori_loop(0, kernels, forward, 0)
        resist = jax.nn.sigmoid(resist_slope * (inten_scr[...] - resist_level))
        comb = comb_ref[0]
        target_on = (comb > 0).astype(f32)
        weight_abs = jnp.abs(comb)
        error_term = 2.0 * resist_slope * weight_abs * (resist - target_on) * resist * (1.0 - resist)
        err_scr[...] = 2.0 * error_term
        lax.fori_loop(0, kernels, backward, 0)
        damp = mm3(dcat_scr[...], t2h, t2l)
        damp_re = damp[:, :lane]
        damp_im = damp[:, lane:]
        t_re = pre * damp_re + pim * damp_im
        t_im = pre * damp_im - pim * damp_re
        dspec_re = t_re[:freq]
        dspec_im = t_im[:freq]
        for i in range(1, kernels):
            dspec_re = dspec_re + t_re[i * freq:(i + 1) * freq]
            dspec_im = dspec_im + t_im[i * freq:(i + 1) * freq]
        dcross = jnp.concatenate(
            [
                jnp.concatenate([dspec_re, -dspec_im], axis=1),
                jnp.concatenate([-dspec_im, -dspec_re], axis=1),
            ],
            axis=0,
        )
        dupper = mm3(dcross, t3h, t3l) / norm_area
        dmask = dot(bt_ref[...], dupper.astype(bf16))
        grad_logit = dmask * mask_soft * (1.0 - mask_soft)
        step_scale = lax.rsqrt(jnp.mean(grad_logit * grad_logit) + 1e-06)
        logit_scr[...] = logit - step_rate * step_scale * grad_logit
        return carry

    lax.fori_loop(0, steps_ref[pl.program_id(0)], update, 0)
    out_ref[0] = logit_scr[MARGIN:MARGIN + CORE, MARGIN:MARGIN + CORE]


def lane_pad(x, width):
    return jnp.pad(x, ((0, 0), (0, width - x.shape[1])))


def row_pad(x, height):
    return jnp.pad(x, ((0, height - x.shape[0]), (0, 0)))


def tiles_call(steps, kernel_weight, logit_tiles, comb_tiles, pupil_spectra, cosine_table, sine_table):
    tiles = logit_tiles.shape[0]
    kernels = pupil_spectra.shape[1]
    freq, side = cosine_table.shape
    lane = 128
    basis_full = jnp.concatenate([cosine_table, sine_table], axis=0)
    basis_bf = basis_full.astype(jnp.bfloat16)
    cos_t = cosine_table.T
    sin_t = sine_table.T
    pre = lane_pad(pupil_spectra[0].reshape(kernels * freq, freq), lane)
    pim = lane_pad(pupil_spectra[1].reshape(kernels * freq, freq), lane)
    t1 = jnp.concatenate([lane_pad(cos_t, lane), lane_pad(sin_t, lane)], axis=1)
    wv = jnp.concatenate(
        [
            row_pad(jnp.concatenate([cosine_table, sine_table], axis=1), lane),
            row_pad(jnp.concatenate([-sine_table, cosine_table], axis=1), lane),
        ],
        axis=0,
    )
    t2 = jnp.concatenate(
        [
            jnp.concatenate([lane_pad(cos_t, lane), lane_pad(-sin_t, lane)], axis=1),
            jnp.concatenate([lane_pad(sin_t, lane), lane_pad(cos_t, lane)], axis=1),
        ],
        axis=0,
    )
    t3 = jnp.concatenate([row_pad(cosine_table, lane), row_pad(sine_table, lane)], axis=0)
    tables = [t1, wv, t2, t3]
    consts = [pre, pim, basis_bf.T, basis_bf] + tables
    smem = pl.BlockSpec(memory_space=pltpu.MemorySpace.SMEM)
    tile_spec = pl.BlockSpec((1, side, side), lambda t: (t, 0, 0))
    const_specs = [pl.BlockSpec(c.shape, lambda t: (0, 0)) for c in consts]
    split_scratch = []
    for table in tables:
        split_scratch += [pltpu.VMEM(table.shape, jnp.bfloat16)] * 2
    return pl.pallas_call(
        tile_kernel,
        grid=(tiles,),
        out_shape=jax.ShapeDtypeStruct((tiles, CORE, CORE), jnp.float32),
        in_specs=[smem, smem, tile_spec, tile_spec] + const_specs,
        out_specs=pl.BlockSpec((1, CORE, CORE), lambda t: (t, 0, 0)),
        scratch_shapes=[pltpu.VMEM((side, side), jnp.float32)]
        + split_scratch
        + [
            pltpu.VMEM((kernels * freq, side), jnp.bfloat16),
            pltpu.VMEM((kernels * freq, side), jnp.bfloat16),
            pltpu.VMEM((kernels, 2, side, side), jnp.float32),
            pltpu.VMEM((side, side), jnp.float32),
            pltpu.VMEM((side, side), jnp.float32),
            pltpu.VMEM((kernels * freq, 2 * side), jnp.float32),
        ],
        compiler_params=pltpu.CompilerParams(vmem_limit_bytes=56 * 1024 * 1024),
    )(steps, kernel_weight, logit_tiles, comb_tiles, *consts)


def on_device(mask_logit, target, pixel_weight, tile_steps, pupil_spectra, kernel_weight):
    cosine_table, sine_table = spectral_tables(TILE, KF)
    combined = jnp.where(target == 1, pixel_weight, -pixel_weight)
    tiles_dev = mask_logit.shape[1] // CORE

    def cut_tiles(extended):
        widened = jnp.pad(extended, ((0, 0), (MARGIN, MARGIN)))
        return jnp.stack(
            [widened[:, column * CORE : column * CORE + TILE] for column in range(tiles_dev)]
        )

    state_field = mask_logit
    for round_index in range(ROUNDS):
        both_ext = extended_2(jnp.stack([state_field, combined]), (("row", 1),), MARGIN)
        logit_tiles = cut_tiles(both_ext[0])
        comb_tiles = cut_tiles(both_ext[1])
        own_steps = tile_steps[round_index, 0]
        own_cores = tiles_call(
            own_steps, kernel_weight, logit_tiles, comb_tiles, pupil_spectra, cosine_table, sine_table
        )
        state_field = jnp.transpose(own_cores, (1, 0, 2)).reshape(CORE, tiles_dev * CORE)
    return state_field


def solution(mesh):
    return jax.shard_map(
        on_device,
        mesh=mesh,
        in_specs=(
            P(("grp", "row"), None),
            P(("grp", "row"), None),
            P(("grp", "row"), None),
            P(None, ("grp", "row"), None),
            P(),
            P(),
        ),
        out_specs=P(("grp", "row"), None),
        check_vma=False,
    )
```

```python
import math

import jax
import jax.numpy as jnp
from jax import lax
from jax.experimental import pallas as pl
from jax.experimental.pallas import tpu as pltpu
from jax.sharding import PartitionSpec as P

CORE = 128
MARGIN = 128
KF = 32
ROUNDS = 2
TILE = 384


resist_slope = 4.0
resist_level = 1.0
step_rate = 0.1


def extended_2(shard, sides, width):
    for axis, dim in sides:
        size, length = (lax.axis_size(axis), shard.shape[dim])
        up = [(i, (i + 1) % size) for i in range(size - 1)]
        down = [(j, i) for i, j in up]
        last = lax.slice_in_dim(shard, length - width, length, axis=dim)
        first = lax.slice_in_dim(shard, 0, width, axis=dim)
        before = lax.ppermute(last, axis, up)
        after = lax.ppermute(first, axis, down)
        shard = jnp.concatenate([before, shard, after], axis=dim)
    return shard


def spectral_tables(side_len, freq_count):
    freq_values = jnp.arange(freq_count, dtype=jnp.int32) - freq_count // 2
    pixel_pos = jnp.arange(side_len, dtype=jnp.int32)
    phase_idx = jnp.mod(freq_values[:, None] * pixel_pos[None, :], side_len)
    angles = phase_idx.astype(jnp.float32) * (2.0 * math.pi / side_len)
    return (jnp.cos(angles), jnp.sin(angles))


def split_bf(x):
    hi = x.astype(jnp.bfloat16)
    lo = (x - hi.astype(jnp.float32)).astype(jnp.bfloat16)
    return hi, lo


def tile_kernel(
    steps_ref, w_ref, logit_ref, comb_ref, pre_ref, pim_ref, bt_ref, b_ref, t1_ref, wv_ref, t2_ref,
    t3_ref, out_ref, logit_scr, t1c, wvc, t2c, t3c, wre_scr, wim_scr,
    field_scr, inten_scr, err_scr, dcat_scr,
):
    kernels = field_scr.shape[0]
    side = field_scr.shape[2]
    freq = wre_scr.shape[0] // kernels
    lane = pre_ref.shape[1]
    norm_area = float(side * side)
    f32 = jnp.float32
    bf16 = jnp.bfloat16

    def dot(a, b):
        return jnp.dot(a, b, preferred_element_type=f32)

    for table, cat_ref in ((t1_ref, t1c), (wv_ref, wvc), (t2_ref, t2c), (t3_ref, t3c)):
        hi, lo = split_bf(table[...])
        depth = table.shape[0]
        cat_ref[:depth] = hi
        cat_ref[depth:2 * depth] = hi
        cat_ref[2 * depth:] = lo

    def mm3(x, cat_ref):
        x_hi, x_lo = split_bf(x)
        return dot(jnp.concatenate([x_hi, x_lo, x_hi], axis=1), cat_ref[...])

    logit_scr[...] = logit_ref[0]

    def forward(k, carry):
        r0 = pl.multiple_of(k * freq, freq)
        a0 = wre_scr[pl.ds(r0, freq), :]
        a1 = wim_scr[pl.ds(r0, freq), :]
        c0 = jnp.concatenate([a0, -a1], axis=0)
        c1 = jnp.concatenate([a1, a0], axis=0)
        basis_t = bt_ref[...]
        f_re = dot(basis_t, c0).astype(bf16).astype(f32)
        f_im = dot(basis_t, c1).astype(bf16).astype(f32)
        field_scr[k, 0] = f_re
        field_scr[k, 1] = f_im
        inten_scr[...] += w_ref[k] * (f_re * f_re + f_im * f_im)
        return carry

    def backward(k, carry):
        scale = w_ref[k] * err_scr[...]
        basis = b_ref[...]
        g_re = (scale * field_scr[k, 0]).astype(bf16)
        g_im = (scale * field_scr[k, 1]).astype(bf16)
        p_re = dot(basis, g_re)
        p_im = dot(basis, g_im)
        r0 = pl.multiple_of(k * freq, freq)
        dcat_scr[pl.ds(r0, freq), :side] = p_re[:freq] + p_im[freq:]
        dcat_scr[pl.ds(r0, freq), side:] = p_im[:freq] - p_re[freq:]
        return carry

    def update(step, carry):
        logit = logit_scr[...]
        mask_soft = jax.nn.sigmoid(logit)
        upper = dot(b_ref[...], mask_soft.astype(bf16))
        cross = mm3(upper, t1c) / norm_area
        spec_re = cross[:freq, :lane] - cross[freq:, lane:]
        spec_im = -(cross[:freq, lane:] + cross[freq:, :lane])
        sre = jnp.concatenate([spec_re] * kernels, axis=0)
        sim = jnp.concatenate([spec_im] * kernels, axis=0)
        pre = pre_ref[...]
        pim = pim_ref[...]
        amp_re = pre * sre - pim * sim
        amp_im = pre * sim + pim * sre
        waves = mm3(jnp.concatenate([amp_re, amp_im], axis=1), wvc)
        wre_scr[...] = waves[:, :side].astype(bf16)
        wim_scr[...] = waves[:, side:].astype(bf16)
        inten_scr[...] = jnp.zeros_like(inten_scr)
        lax.fori_loop(0, kernels, forward, 0, unroll=2)
        resist = jax.nn.sigmoid(resist_slope * (inten_scr[...] - resist_level))
        comb = comb_ref[0]
        target_on = (comb > 0).astype(f32)
        weight_abs = jnp.abs(comb)
        error_term = 2.0 * resist_slope * weight_abs * (resist - target_on) * resist * (1.0 - resist)
        err_scr[...] = 2.0 * error_term
        lax.fori_loop(0, kernels, backward, 0, unroll=2)
        damp = mm3(dcat_scr[...], t2c)
        damp_re = damp[:, :lane]
        damp_im = damp[:, lane:]
        t_re = pre * damp_re + pim * damp_im
        t_im = pre * damp_im - pim * damp_re
        dspec_re = t_re[:freq]
        dspec_im = t_im[:freq]
        for i in range(1, kernels):
            dspec_re = dspec_re + t_re[i * freq:(i + 1) * freq]
            dspec_im = dspec_im + t_im[i * freq:(i + 1) * freq]
        dcross = jnp.concatenate(
            [
                jnp.concatenate([dspec_re, -dspec_im], axis=1),
                jnp.concatenate([-dspec_im, -dspec_re], axis=1),
            ],
            axis=0,
        )
        dupper = mm3(dcross, t3c) / norm_area
        dmask = dot(bt_ref[...], dupper.astype(bf16))
        grad_logit = dmask * mask_soft * (1.0 - mask_soft)
        step_scale = lax.rsqrt(jnp.mean(grad_logit * grad_logit) + 1e-06)
        logit_scr[...] = logit - step_rate * step_scale * grad_logit
        return carry

    lax.fori_loop(0, steps_ref[pl.program_id(0)], update, 0)
    out_ref[0] = logit_scr[MARGIN:MARGIN + CORE, MARGIN:MARGIN + CORE]


def lane_pad(x, width):
    return jnp.pad(x, ((0, 0), (0, width - x.shape[1])))


def row_pad(x, height):
    return jnp.pad(x, ((0, height - x.shape[0]), (0, 0)))


def tiles_call(steps, kernel_weight, logit_tiles, comb_tiles, pupil_spectra, cosine_table, sine_table):
    tiles = logit_tiles.shape[0]
    kernels = pupil_spectra.shape[1]
    freq, side = cosine_table.shape
    lane = 128
    basis_full = jnp.concatenate([cosine_table, sine_table], axis=0)
    basis_bf = basis_full.astype(jnp.bfloat16)
    cos_t = cosine_table.T
    sin_t = sine_table.T
    pre = lane_pad(pupil_spectra[0].reshape(kernels * freq, freq), lane)
    pim = lane_pad(pupil_spectra[1].reshape(kernels * freq, freq), lane)
    t1 = jnp.concatenate([lane_pad(cos_t, lane), lane_pad(sin_t, lane)], axis=1)
    wv = jnp.concatenate(
        [
            row_pad(jnp.concatenate([cosine_table, sine_table], axis=1), lane),
            row_pad(jnp.concatenate([-sine_table, cosine_table], axis=1), lane),
        ],
        axis=0,
    )
    t2 = jnp.concatenate(
        [
            jnp.concatenate([lane_pad(cos_t, lane), lane_pad(-sin_t, lane)], axis=1),
            jnp.concatenate([lane_pad(sin_t, lane), lane_pad(cos_t, lane)], axis=1),
        ],
        axis=0,
    )
    t3 = jnp.concatenate([row_pad(cosine_table, lane), row_pad(sine_table, lane)], axis=0)
    tables = [t1, wv, t2, t3]
    consts = [pre, pim, basis_bf.T, basis_bf] + tables
    smem = pl.BlockSpec(memory_space=pltpu.MemorySpace.SMEM)
    tile_spec = pl.BlockSpec((1, side, side), lambda t: (t, 0, 0))
    const_specs = [pl.BlockSpec(c.shape, lambda t: (0, 0)) for c in consts]
    split_scratch = []
    for table in tables:
        split_scratch.append(pltpu.VMEM((3 * table.shape[0], table.shape[1]), jnp.bfloat16))
    return pl.pallas_call(
        tile_kernel,
        grid=(tiles,),
        out_shape=jax.ShapeDtypeStruct((tiles, CORE, CORE), jnp.float32),
        in_specs=[smem, smem, tile_spec, tile_spec] + const_specs,
        out_specs=pl.BlockSpec((1, CORE, CORE), lambda t: (t, 0, 0)),
        scratch_shapes=[pltpu.VMEM((side, side), jnp.float32)]
        + split_scratch
        + [
            pltpu.VMEM((kernels * freq, side), jnp.bfloat16),
            pltpu.VMEM((kernels * freq, side), jnp.bfloat16),
            pltpu.VMEM((kernels, 2, side, side), jnp.float32),
            pltpu.VMEM((side, side), jnp.float32),
            pltpu.VMEM((side, side), jnp.float32),
            pltpu.VMEM((kernels * freq, 2 * side), jnp.float32),
        ],
        compiler_params=pltpu.CompilerParams(vmem_limit_bytes=56 * 1024 * 1024),
    )(steps, kernel_weight, logit_tiles, comb_tiles, *consts)


def on_device(mask_logit, target, pixel_weight, tile_steps, pupil_spectra, kernel_weight):
    cosine_table, sine_table = spectral_tables(TILE, KF)
    combined = jnp.where(target == 1, pixel_weight, -pixel_weight)
    tiles_dev = mask_logit.shape[1] // CORE

    def cut_tiles(extended):
        widened = jnp.pad(extended, ((0, 0), (MARGIN, MARGIN)))
        return jnp.stack(
            [widened[:, column * CORE : column * CORE + TILE] for column in range(tiles_dev)]
        )

    state_field = mask_logit
    for round_index in range(ROUNDS):
        both_ext = extended_2(jnp.stack([state_field, combined]), (("row", 1),), MARGIN)
        logit_tiles = cut_tiles(both_ext[0])
        comb_tiles = cut_tiles(both_ext[1])
        own_steps = tile_steps[round_index, 0]
        own_cores = tiles_call(
            own_steps, kernel_weight, logit_tiles, comb_tiles, pupil_spectra, cosine_table, sine_table
        )
        state_field = jnp.transpose(own_cores, (1, 0, 2)).reshape(CORE, tiles_dev * CORE)
    return state_field


def solution(mesh):
    return jax.shard_map(
        on_device,
        mesh=mesh,
        in_specs=(
            P(("grp", "row"), None),
            P(("grp", "row"), None),
            P(("grp", "row"), None),
            P(None, ("grp", "row"), None),
            P(),
            P(),
        ),
        out_specs=P(("grp", "row"), None),
        check_vma=False,
    )
```

```python
import math

import jax
import numpy as np
import jax.numpy as jnp
from jax import lax
from jax.experimental import pallas as pl
from jax.experimental.pallas import tpu as pltpu
from jax.sharding import PartitionSpec as P

CORE = 128
MARGIN = 128
KF = 32
ROUNDS = 2
TILE = 384


resist_slope = 4.0
resist_level = 1.0
step_rate = 0.1


def extended_2(shard, sides, width):
    for axis, dim in sides:
        size, length = (lax.axis_size(axis), shard.shape[dim])
        up = [(i, (i + 1) % size) for i in range(size - 1)]
        down = [(j, i) for i, j in up]
        last = lax.slice_in_dim(shard, length - width, length, axis=dim)
        first = lax.slice_in_dim(shard, 0, width, axis=dim)
        before = lax.ppermute(last, axis, up)
        after = lax.ppermute(first, axis, down)
        shard = jnp.concatenate([before, shard, after], axis=dim)
    return shard


def spectral_tables(side_len, freq_count):
    freq_values = jnp.arange(freq_count, dtype=jnp.int32) - freq_count // 2
    pixel_pos = jnp.arange(side_len, dtype=jnp.int32)
    phase_idx = jnp.mod(freq_values[:, None] * pixel_pos[None, :], side_len)
    angles = phase_idx.astype(jnp.float32) * (2.0 * math.pi / side_len)
    return (jnp.cos(angles), jnp.sin(angles))


def split_bf(x):
    hi = x.astype(jnp.bfloat16)
    lo = (x - hi.astype(jnp.float32)).astype(jnp.bfloat16)
    return hi, lo


def tile_kernel(
    steps_ref, w_ref, logit_ref, comb_ref, pupil_ref, bt_ref, b_ref, t1_ref, wv_ref, t2_ref,
    t3_ref, out_ref, logit_scr, comb_scr, pre_ref, pim_ref, t1c, wvc, t2c, t3c, wre_scr, wim_scr,
    field_scr, inten_scr, err_scr, dcat_scr,
):
    kernels = field_scr.shape[0]
    side = field_scr.shape[2]
    freq = wre_scr.shape[0] // kernels
    lane = pre_ref.shape[1]
    norm_area = float(side * side)
    f32 = jnp.float32
    bf16 = jnp.bfloat16

    def dot(a, b):
        return jnp.dot(a, b, preferred_element_type=f32)

    for table, cat_ref in ((t1_ref, t1c), (wv_ref, wvc), (t2_ref, t2c), (t3_ref, t3c)):
        hi, lo = split_bf(table[...])
        depth = table.shape[0]
        cat_ref[:depth] = hi
        cat_ref[depth:2 * depth] = hi
        cat_ref[2 * depth:] = lo

    def mm3(x, cat_ref):
        x_hi, x_lo = split_bf(x)
        return dot(jnp.concatenate([x_hi, x_lo, x_hi], axis=1), cat_ref[...])

    tile = pl.program_id(0)
    width = logit_ref.shape[1]
    for column in range(width // CORE):

        @pl.when(tile == column)
        def _():
            start = column * CORE - MARGIN
            src_lo = max(start, 0)
            src_hi = min(start + side, width)
            for dst, src in ((logit_scr, logit_ref), (comb_scr, comb_ref)):
                if src_lo > start:
                    dst[:, : src_lo - start] = jnp.zeros((side, src_lo - start), f32)
                if src_hi < start + side:
                    dst[:, src_hi - start :] = jnp.zeros((side, start + side - src_hi), f32)
                dst[:, src_lo - start : src_hi - start] = src[:, src_lo:src_hi]

    for pad_ref, part in ((pre_ref, 0), (pim_ref, 1)):
        pad_ref[...] = jnp.zeros_like(pad_ref)
        pad_ref[:, :freq] = pupil_ref[part]

    def forward(k, carry):
        r0 = pl.multiple_of(k * freq, freq)
        a0 = wre_scr[pl.ds(r0, freq), :]
        a1 = wim_scr[pl.ds(r0, freq), :]
        c0 = jnp.concatenate([a0, -a1], axis=0)
        c1 = jnp.concatenate([a1, a0], axis=0)
        basis_t = bt_ref[...]
        f_re = dot(basis_t, c0).astype(bf16).astype(f32)
        f_im = dot(basis_t, c1).astype(bf16).astype(f32)
        field_scr[k, 0] = f_re
        field_scr[k, 1] = f_im
        inten_scr[...] += w_ref[k] * (f_re * f_re + f_im * f_im)
        return carry

    def backward(k, carry):
        scale = w_ref[k] * err_scr[...]
        basis = b_ref[...]
        g_re = (scale * field_scr[k, 0]).astype(bf16)
        g_im = (scale * field_scr[k, 1]).astype(bf16)
        p_re = dot(basis, g_re)
        p_im = dot(basis, g_im)
        r0 = pl.multiple_of(k * freq, freq)
        dcat_scr[pl.ds(r0, freq), :side] = p_re[:freq] + p_im[freq:]
        dcat_scr[pl.ds(r0, freq), side:] = p_im[:freq] - p_re[freq:]
        return carry

    def update(step, carry):
        logit = logit_scr[...]
        mask_soft = jax.nn.sigmoid(logit)
        upper = dot(b_ref[...], mask_soft.astype(bf16))
        cross = mm3(upper, t1c) / norm_area
        spec_re = cross[:freq, :lane] - cross[freq:, lane:]
        spec_im = -(cross[:freq, lane:] + cross[freq:, :lane])
        sre = jnp.concatenate([spec_re] * kernels, axis=0)
        sim = jnp.concatenate([spec_im] * kernels, axis=0)
        pre = pre_ref[...]
        pim = pim_ref[...]
        amp_re = pre * sre - pim * sim
        amp_im = pre * sim + pim * sre
        waves = mm3(jnp.concatenate([amp_re, amp_im], axis=1), wvc)
        wre_scr[...] = waves[:, :side].astype(bf16)
        wim_scr[...] = waves[:, side:].astype(bf16)
        inten_scr[...] = jnp.zeros_like(inten_scr)
        lax.fori_loop(0, kernels, forward, 0, unroll=2)
        resist = jax.nn.sigmoid(resist_slope * (inten_scr[...] - resist_level))
        comb = comb_scr[...]
        target_on = (comb > 0).astype(f32)
        weight_abs = jnp.abs(comb)
        error_term = 2.0 * resist_slope * weight_abs * (resist - target_on) * resist * (1.0 - resist)
        err_scr[...] = 2.0 * error_term
        lax.fori_loop(0, kernels, backward, 0, unroll=2)
        damp = mm3(dcat_scr[...], t2c)
        damp_re = damp[:, :lane]
        damp_im = damp[:, lane:]
        t_re = pre * damp_re + pim * damp_im
        t_im = pre * damp_im - pim * damp_re
        dspec_re = t_re[:freq]
        dspec_im = t_im[:freq]
        for i in range(1, kernels):
            dspec_re = dspec_re + t_re[i * freq:(i + 1) * freq]
            dspec_im = dspec_im + t_im[i * freq:(i + 1) * freq]
        dcross = jnp.concatenate(
            [
                jnp.concatenate([dspec_re, -dspec_im], axis=1),
                jnp.concatenate([-dspec_im, -dspec_re], axis=1),
            ],
            axis=0,
        )
        dupper = mm3(dcross, t3c) / norm_area
        dmask = dot(bt_ref[...], dupper.astype(bf16))
        grad_logit = dmask * mask_soft * (1.0 - mask_soft)
        step_scale = lax.rsqrt(jnp.mean(grad_logit * grad_logit) + 1e-06)
        logit_scr[...] = logit - step_rate * step_scale * grad_logit
        return carry

    lax.fori_loop(0, steps_ref[pl.program_id(0)], update, 0)
    out_ref[...] = logit_scr[MARGIN:MARGIN + CORE, MARGIN:MARGIN + CORE]


def lane_pad(x, width):
    return np.pad(x, ((0, 0), (0, width - x.shape[1])))


def row_pad(x, height):
    return np.pad(x, ((0, height - x.shape[0]), (0, 0)))


def spectral_constants(side_len, freq_count, lane):
    freq_values = np.arange(freq_count, dtype=np.int64) - freq_count // 2
    pixel_pos = np.arange(side_len, dtype=np.int64)
    phase_idx = np.mod(freq_values[:, None] * pixel_pos[None, :], side_len)
    angles = phase_idx.astype(np.float32) * np.float32(2.0 * math.pi / side_len)
    cos_tab = np.cos(angles.astype(np.float64)).astype(np.float32)
    sin_tab = np.sin(angles.astype(np.float64)).astype(np.float32)
    cos_t = cos_tab.T
    sin_t = sin_tab.T
    t1 = np.concatenate([lane_pad(cos_t, lane), lane_pad(sin_t, lane)], axis=1)
    wv = np.concatenate(
        [
            row_pad(np.concatenate([cos_tab, sin_tab], axis=1), lane),
            row_pad(np.concatenate([-sin_tab, cos_tab], axis=1), lane),
        ],
        axis=0,
    )
    t2 = np.concatenate(
        [
            np.concatenate([lane_pad(cos_t, lane), lane_pad(-sin_t, lane)], axis=1),
            np.concatenate([lane_pad(sin_t, lane), lane_pad(cos_t, lane)], axis=1),
        ],
        axis=0,
    )
    t3 = np.concatenate([row_pad(cos_tab, lane), row_pad(sin_tab, lane)], axis=0)
    basis_full = np.concatenate([cos_tab, sin_tab], axis=0)
    return basis_full, [t1, wv, t2, t3]


def tiles_call(steps, kernel_weight, logit_ext, comb_ext, pupil_spectra):
    rows, width = logit_ext.shape
    kernels = pupil_spectra.shape[1]
    freq, side, lane = KF, TILE, 128
    basis_full, tables = spectral_constants(side, freq, lane)
    basis_bf = jnp.asarray(basis_full).astype(jnp.bfloat16)
    tables = [jnp.asarray(t) for t in tables]
    pupil = pupil_spectra.reshape(2, kernels * freq, freq)
    consts = [pupil, basis_bf.T, basis_bf] + tables
    smem = pl.BlockSpec(memory_space=pltpu.MemorySpace.SMEM)
    ext_spec = pl.BlockSpec((rows, width), lambda t: (0, 0))
    const_specs = [pl.BlockSpec(c.shape, lambda t, n=c.ndim: (0,) * n) for c in consts]
    split_scratch = []
    for table in tables:
        split_scratch.append(pltpu.VMEM((3 * table.shape[0], table.shape[1]), jnp.bfloat16))
    return pl.pallas_call(
        tile_kernel,
        grid=(width // CORE,),
        out_shape=jax.ShapeDtypeStruct((CORE, width), jnp.float32),
        in_specs=[smem, smem, ext_spec, ext_spec] + const_specs,
        out_specs=pl.BlockSpec((CORE, CORE), lambda t: (0, t)),
        scratch_shapes=[
            pltpu.VMEM((side, side), jnp.float32),
            pltpu.VMEM((side, side), jnp.float32),
            pltpu.VMEM((kernels * freq, lane), jnp.float32),
            pltpu.VMEM((kernels * freq, lane), jnp.float32),
        ]
        + split_scratch
        + [
            pltpu.VMEM((kernels * freq, side), jnp.bfloat16),
            pltpu.VMEM((kernels * freq, side), jnp.bfloat16),
            pltpu.VMEM((kernels, 2, side, side), jnp.float32),
            pltpu.VMEM((side, side), jnp.float32),
            pltpu.VMEM((side, side), jnp.float32),
            pltpu.VMEM((kernels * freq, 2 * side), jnp.float32),
        ],
        compiler_params=pltpu.CompilerParams(vmem_limit_bytes=56 * 1024 * 1024),
    )(steps, kernel_weight, logit_ext, comb_ext, *consts)


def on_device(mask_logit, target, pixel_weight, tile_steps, pupil_spectra, kernel_weight):
    combined = jnp.where(target == 1, pixel_weight, -pixel_weight)
    state_field = mask_logit
    comb_ext = None
    for round_index in range(ROUNDS):
        if comb_ext is None:
            both_ext = extended_2(jnp.stack([state_field, combined]), (("row", 1),), MARGIN)
            logit_ext, comb_ext = both_ext[0], both_ext[1]
        else:
            logit_ext = extended_2(state_field, (("row", 0),), MARGIN)
        own_steps = tile_steps[round_index, 0]
        state_field = tiles_call(own_steps, kernel_weight, logit_ext, comb_ext, pupil_spectra)
    return state_field


def solution(mesh):
    return jax.shard_map(
        on_device,
        mesh=mesh,
        in_specs=(
            P(("grp", "row"), None),
            P(("grp", "row"), None),
            P(("grp", "row"), None),
            P(None, ("grp", "row"), None),
            P(),
            P(),
        ),
        out_specs=P(("grp", "row"), None),
        check_vma=False,
    )
```

```python
import math

import jax
import numpy as np
import jax.numpy as jnp
from jax import lax
from jax.experimental import pallas as pl
from jax.experimental.pallas import tpu as pltpu
from jax.sharding import PartitionSpec as P

CORE = 128
MARGIN = 128
KF = 32
ROUNDS = 2
TILE = 384


resist_slope = 4.0
resist_level = 1.0
step_rate = 0.1


def extended_2(shard, sides, width):
    for axis, dim in sides:
        size, length = (lax.axis_size(axis), shard.shape[dim])
        up = [(i, (i + 1) % size) for i in range(size - 1)]
        down = [(j, i) for i, j in up]
        last = lax.slice_in_dim(shard, length - width, length, axis=dim)
        first = lax.slice_in_dim(shard, 0, width, axis=dim)
        before = lax.ppermute(last, axis, up)
        after = lax.ppermute(first, axis, down)
        shard = jnp.concatenate([before, shard, after], axis=dim)
    return shard


def spectral_tables(side_len, freq_count):
    freq_values = jnp.arange(freq_count, dtype=jnp.int32) - freq_count // 2
    pixel_pos = jnp.arange(side_len, dtype=jnp.int32)
    phase_idx = jnp.mod(freq_values[:, None] * pixel_pos[None, :], side_len)
    angles = phase_idx.astype(jnp.float32) * (2.0 * math.pi / side_len)
    return (jnp.cos(angles), jnp.sin(angles))


def split_bf(x):
    hi = x.astype(jnp.bfloat16)
    lo = (x - hi.astype(jnp.float32)).astype(jnp.bfloat16)
    return hi, lo


def tile_kernel(
    steps_ref, w_ref, logit_ref, comb_ref, pupil_ref, bt_ref, b_ref, t1_ref, wv_ref, t2_ref,
    t3_ref, out_ref, logit_scr, comb_scr, pre_ref, pim_ref, t1c, wvc, t2c, t3c, wre_scr, wim_scr,
    field_scr, inten_scr, err_scr, dcat_scr,
):
    kernels = field_scr.shape[0]
    side = field_scr.shape[2]
    freq = wre_scr.shape[0] // kernels
    lane = pre_ref.shape[1]
    norm_area = float(side * side)
    f32 = jnp.float32
    bf16 = jnp.bfloat16

    def dot(a, b):
        return jnp.dot(a, b, preferred_element_type=f32)

    for table, cat_ref in ((t1_ref, t1c), (wv_ref, wvc), (t2_ref, t2c), (t3_ref, t3c)):
        hi, lo = split_bf(table[...])
        depth = table.shape[0]
        cat_ref[:depth] = hi
        cat_ref[depth:2 * depth] = hi
        cat_ref[2 * depth:] = lo

    def mm3(x, cat_ref):
        x_hi, x_lo = split_bf(x)
        return dot(jnp.concatenate([x_hi, x_lo, x_hi], axis=1), cat_ref[...])

    tile = pl.program_id(0)
    width = logit_ref.shape[1]
    for column in range(width // CORE):

        @pl.when(tile == column)
        def _():
            start = column * CORE - MARGIN
            src_lo = max(start, 0)
            src_hi = min(start + side, width)
            for dst, src in ((logit_scr, logit_ref), (comb_scr, comb_ref)):
                if src_lo > start:
                    dst[:, : src_lo - start] = jnp.zeros((side, src_lo - start), f32)
                if src_hi < start + side:
                    dst[:, src_hi - start :] = jnp.zeros((side, start + side - src_hi), f32)
                dst[:, src_lo - start : src_hi - start] = src[:, src_lo:src_hi]

    for pad_ref, part in ((pre_ref, 0), (pim_ref, 1)):
        pad_ref[...] = jnp.zeros_like(pad_ref)
        pad_ref[:, :freq] = pupil_ref[part]

    def forward(k, carry):
        r0 = pl.multiple_of(k * freq, freq)
        a0 = wre_scr[pl.ds(r0, freq), :]
        a1 = wim_scr[pl.ds(r0, freq), :]
        c0 = jnp.concatenate([a0, -a1], axis=0)
        c1 = jnp.concatenate([a1, a0], axis=0)
        basis_t = bt_ref[...]
        f_re = dot(basis_t, c0).astype(bf16).astype(f32)
        f_im = dot(basis_t, c1).astype(bf16).astype(f32)
        field_scr[k, 0] = f_re
        field_scr[k, 1] = f_im
        inten_scr[...] += w_ref[k] * (f_re * f_re + f_im * f_im)
        return carry

    def backward(k, carry):
        scale = w_ref[k] * err_scr[...]
        basis = b_ref[...]
        g_re = (scale * field_scr[k, 0]).astype(bf16)
        g_im = (scale * field_scr[k, 1]).astype(bf16)
        p_re = dot(basis, g_re)
        p_im = dot(basis, g_im)
        r0 = pl.multiple_of(k * freq, freq)
        dcat_scr[pl.ds(r0, freq), :side] = p_re[:freq] + p_im[freq:]
        dcat_scr[pl.ds(r0, freq), side:] = p_im[:freq] - p_re[freq:]
        return carry

    def update(step, carry):
        logit = logit_scr[...]
        mask_soft = jax.nn.sigmoid(logit)
        upper = dot(b_ref[...], mask_soft.astype(bf16))
        cross = mm3(upper, t1c) / norm_area
        spec_re = cross[:freq, :lane] - cross[freq:, lane:]
        spec_im = -(cross[:freq, lane:] + cross[freq:, :lane])
        sre = jnp.concatenate([spec_re] * kernels, axis=0)
        sim = jnp.concatenate([spec_im] * kernels, axis=0)
        pre = pre_ref[...]
        pim = pim_ref[...]
        amp_re = pre * sre - pim * sim
        amp_im = pre * sim + pim * sre
        waves = mm3(jnp.concatenate([amp_re, amp_im], axis=1), wvc)
        wre_scr[...] = waves[:, :side].astype(bf16)
        wim_scr[...] = waves[:, side:].astype(bf16)
        inten_scr[...] = jnp.zeros_like(inten_scr)
        lax.fori_loop(0, kernels, forward, 0, unroll=6)
        resist = jax.nn.sigmoid(resist_slope * (inten_scr[...] - resist_level))
        comb = comb_scr[...]
        target_on = (comb > 0).astype(f32)
        weight_abs = jnp.abs(comb)
        error_term = 2.0 * resist_slope * weight_abs * (resist - target_on) * resist * (1.0 - resist)
        err_scr[...] = 2.0 * error_term
        lax.fori_loop(0, kernels, backward, 0, unroll=6)
        damp = mm3(dcat_scr[...], t2c)
        damp_re = damp[:, :lane]
        damp_im = damp[:, lane:]
        t_re = pre * damp_re + pim * damp_im
        t_im = pre * damp_im - pim * damp_re
        dspec_re = t_re[:freq]
        dspec_im = t_im[:freq]
        for i in range(1, kernels):
            dspec_re = dspec_re + t_re[i * freq:(i + 1) * freq]
            dspec_im = dspec_im + t_im[i * freq:(i + 1) * freq]
        dcross = jnp.concatenate(
            [
                jnp.concatenate([dspec_re, -dspec_im], axis=1),
                jnp.concatenate([-dspec_im, -dspec_re], axis=1),
            ],
            axis=0,
        )
        dupper = mm3(dcross, t3c) / norm_area
        dmask = dot(bt_ref[...], dupper.astype(bf16))
        grad_logit = dmask * mask_soft * (1.0 - mask_soft)
        step_scale = lax.rsqrt(jnp.mean(grad_logit * grad_logit) + 1e-06)
        logit_scr[...] = logit - step_rate * step_scale * grad_logit
        return carry

    lax.fori_loop(0, steps_ref[pl.program_id(0)], update, 0)
    out_ref[...] = logit_scr[MARGIN:MARGIN + CORE, MARGIN:MARGIN + CORE]


def lane_pad(x, width):
    return np.pad(x, ((0, 0), (0, width - x.shape[1])))


def row_pad(x, height):
    return np.pad(x, ((0, height - x.shape[0]), (0, 0)))


def spectral_constants(side_len, freq_count, lane):
    freq_values = np.arange(freq_count, dtype=np.int64) - freq_count // 2
    pixel_pos = np.arange(side_len, dtype=np.int64)
    phase_idx = np.mod(freq_values[:, None] * pixel_pos[None, :], side_len)
    angles = phase_idx.astype(np.float32) * np.float32(2.0 * math.pi / side_len)
    cos_tab = np.cos(angles.astype(np.float64)).astype(np.float32)
    sin_tab = np.sin(angles.astype(np.float64)).astype(np.float32)
    cos_t = cos_tab.T
    sin_t = sin_tab.T
    t1 = np.concatenate([lane_pad(cos_t, lane), lane_pad(sin_t, lane)], axis=1)
    wv = np.concatenate(
        [
            row_pad(np.concatenate([cos_tab, sin_tab], axis=1), lane),
            row_pad(np.concatenate([-sin_tab, cos_tab], axis=1), lane),
        ],
        axis=0,
    )
    t2 = np.concatenate(
        [
            np.concatenate([lane_pad(cos_t, lane), lane_pad(-sin_t, lane)], axis=1),
            np.concatenate([lane_pad(sin_t, lane), lane_pad(cos_t, lane)], axis=1),
        ],
        axis=0,
    )
    t3 = np.concatenate([row_pad(cos_tab, lane), row_pad(sin_tab, lane)], axis=0)
    basis_full = np.concatenate([cos_tab, sin_tab], axis=0)
    return basis_full, [t1, wv, t2, t3]


def tiles_call(steps, kernel_weight, logit_ext, comb_ext, pupil_spectra):
    rows, width = logit_ext.shape
    kernels = pupil_spectra.shape[1]
    freq, side, lane = KF, TILE, 128
    basis_full, tables = spectral_constants(side, freq, lane)
    basis_bf = jnp.asarray(basis_full).astype(jnp.bfloat16)
    tables = [jnp.asarray(t) for t in tables]
    pupil = pupil_spectra.reshape(2, kernels * freq, freq)
    consts = [pupil, basis_bf.T, basis_bf] + tables
    smem = pl.BlockSpec(memory_space=pltpu.MemorySpace.SMEM)
    ext_spec = pl.BlockSpec((rows, width), lambda t: (0, 0))
    const_specs = [pl.BlockSpec(c.shape, lambda t, n=c.ndim: (0,) * n) for c in consts]
    split_scratch = []
    for table in tables:
        split_scratch.append(pltpu.VMEM((3 * table.shape[0], table.shape[1]), jnp.bfloat16))
    return pl.pallas_call(
        tile_kernel,
        grid=(width // CORE,),
        out_shape=jax.ShapeDtypeStruct((CORE, width), jnp.float32),
        in_specs=[smem, smem, ext_spec, ext_spec] + const_specs,
        out_specs=pl.BlockSpec((CORE, CORE), lambda t: (0, t)),
        scratch_shapes=[
            pltpu.VMEM((side, side), jnp.float32),
            pltpu.VMEM((side, side), jnp.float32),
            pltpu.VMEM((kernels * freq, lane), jnp.float32),
            pltpu.VMEM((kernels * freq, lane), jnp.float32),
        ]
        + split_scratch
        + [
            pltpu.VMEM((kernels * freq, side), jnp.bfloat16),
            pltpu.VMEM((kernels * freq, side), jnp.bfloat16),
            pltpu.VMEM((kernels, 2, side, side), jnp.float32),
            pltpu.VMEM((side, side), jnp.float32),
            pltpu.VMEM((side, side), jnp.float32),
            pltpu.VMEM((kernels * freq, 2 * side), jnp.float32),
        ],
        compiler_params=pltpu.CompilerParams(vmem_limit_bytes=56 * 1024 * 1024),
    )(steps, kernel_weight, logit_ext, comb_ext, *consts)


def on_device(mask_logit, target, pixel_weight, tile_steps, pupil_spectra, kernel_weight):
    combined = jnp.where(target == 1, pixel_weight, -pixel_weight)
    state_field = mask_logit
    comb_ext = None
    for round_index in range(ROUNDS):
        if comb_ext is None:
            both_ext = extended_2(jnp.stack([state_field, combined]), (("row", 1),), MARGIN)
            logit_ext, comb_ext = both_ext[0], both_ext[1]
        else:
            logit_ext = extended_2(state_field, (("row", 0),), MARGIN)
        own_steps = tile_steps[round_index, 0]
        state_field = tiles_call(own_steps, kernel_weight, logit_ext, comb_ext, pupil_spectra)
    return state_field


def solution(mesh):
    return jax.shard_map(
        on_device,
        mesh=mesh,
        in_specs=(
            P(("grp", "row"), None),
            P(("grp", "row"), None),
            P(("grp", "row"), None),
            P(None, ("grp", "row"), None),
            P(),
            P(),
        ),
        out_specs=P(("grp", "row"), None),
        check_vma=False,
    )
```

```python
import math

import jax
import numpy as np
import jax.numpy as jnp
from jax import lax
from jax.experimental import pallas as pl
from jax.experimental.pallas import tpu as pltpu
from jax.sharding import PartitionSpec as P

CORE = 128
MARGIN = 128
KF = 32
ROUNDS = 2
TILE = 384


resist_slope = 4.0
resist_level = 1.0
step_rate = 0.1


def halo_parts(shard, axis, dim, width):
    size, length = (lax.axis_size(axis), shard.shape[dim])
    up = [(i, (i + 1) % size) for i in range(size - 1)]
    down = [(j, i) for i, j in up]
    last = lax.slice_in_dim(shard, length - width, length, axis=dim)
    first = lax.slice_in_dim(shard, 0, width, axis=dim)
    return lax.ppermute(last, axis, up), lax.ppermute(first, axis, down)


def extended_2(shard, sides, width):
    for axis, dim in sides:
        size, length = (lax.axis_size(axis), shard.shape[dim])
        up = [(i, (i + 1) % size) for i in range(size - 1)]
        down = [(j, i) for i, j in up]
        last = lax.slice_in_dim(shard, length - width, length, axis=dim)
        first = lax.slice_in_dim(shard, 0, width, axis=dim)
        before = lax.ppermute(last, axis, up)
        after = lax.ppermute(first, axis, down)
        shard = jnp.concatenate([before, shard, after], axis=dim)
    return shard


def spectral_tables(side_len, freq_count):
    freq_values = jnp.arange(freq_count, dtype=jnp.int32) - freq_count // 2
    pixel_pos = jnp.arange(side_len, dtype=jnp.int32)
    phase_idx = jnp.mod(freq_values[:, None] * pixel_pos[None, :], side_len)
    angles = phase_idx.astype(jnp.float32) * (2.0 * math.pi / side_len)
    return (jnp.cos(angles), jnp.sin(angles))


def split_bf(x):
    hi = x.astype(jnp.bfloat16)
    lo = (x - hi.astype(jnp.float32)).astype(jnp.bfloat16)
    return hi, lo


def tile_kernel(
    steps_ref, w_ref, lb_ref, lo_ref, la_ref, cb_ref, co_ref, ca_ref, pupil_ref, bt_ref, b_ref, t1_ref, wv_ref, t2_ref,
    t3_ref, out_ref, logit_scr, comb_scr, pre_ref, pim_ref, t1c, wvc, t2c, t3c, wre_scr, wim_scr,
    field_scr, inten_scr, err_scr, dcat_scr,
):
    kernels = field_scr.shape[0]
    side = field_scr.shape[2]
    freq = wre_scr.shape[0] // kernels
    lane = pre_ref.shape[1]
    norm_area = float(side * side)
    f32 = jnp.float32
    bf16 = jnp.bfloat16

    def dot(a, b):
        return jnp.dot(a, b, preferred_element_type=f32)

    for table, cat_ref in ((t1_ref, t1c), (wv_ref, wvc), (t2_ref, t2c), (t3_ref, t3c)):
        hi, lo = split_bf(table[...])
        depth = table.shape[0]
        cat_ref[:depth] = hi
        cat_ref[depth:2 * depth] = hi
        cat_ref[2 * depth:] = lo

    def mm3(x, cat_ref):
        x_hi, x_lo = split_bf(x)
        return dot(jnp.concatenate([x_hi, x_lo, x_hi], axis=1), cat_ref[...])

    tile = pl.program_id(0)
    width = lo_ref.shape[1]
    band = lo_ref.shape[0]
    for column in range(width // CORE):

        @pl.when(tile == column)
        def _():
            start = column * CORE - MARGIN
            src_lo = max(start, 0)
            src_hi = min(start + side, width)
            parts = ((logit_scr, (lb_ref, lo_ref, la_ref)), (comb_scr, (cb_ref, co_ref, ca_ref)))
            for dst, srcs in parts:
                if src_lo > start:
                    dst[:, : src_lo - start] = jnp.zeros((side, src_lo - start), f32)
                if src_hi < start + side:
                    dst[:, src_hi - start :] = jnp.zeros((side, start + side - src_hi), f32)
                for index, src in enumerate(srcs):
                    dst[index * band : (index + 1) * band, src_lo - start : src_hi - start] = src[
                        :, src_lo:src_hi
                    ]

    for pad_ref, part in ((pre_ref, 0), (pim_ref, 1)):
        pad_ref[...] = jnp.zeros_like(pad_ref)
        pad_ref[:, :freq] = pupil_ref[part]

    def forward(k, carry):
        r0 = pl.multiple_of(k * freq, freq)
        a0 = wre_scr[pl.ds(r0, freq), :]
        a1 = wim_scr[pl.ds(r0, freq), :]
        c0 = jnp.concatenate([a0, -a1], axis=0)
        c1 = jnp.concatenate([a1, a0], axis=0)
        basis_t = bt_ref[...]
        f_re = dot(basis_t, c0).astype(bf16).astype(f32)
        f_im = dot(basis_t, c1).astype(bf16).astype(f32)
        field_scr[k, 0] = f_re
        field_scr[k, 1] = f_im
        inten_scr[...] += w_ref[k] * (f_re * f_re + f_im * f_im)
        return carry

    def backward(k, carry):
        scale = w_ref[k] * err_scr[...]
        basis = b_ref[...]
        g_re = (scale * field_scr[k, 0]).astype(bf16)
        g_im = (scale * field_scr[k, 1]).astype(bf16)
        p_re = dot(basis, g_re)
        p_im = dot(basis, g_im)
        r0 = pl.multiple_of(k * freq, freq)
        dcat_scr[pl.ds(r0, freq), :side] = p_re[:freq] + p_im[freq:]
        dcat_scr[pl.ds(r0, freq), side:] = p_im[:freq] - p_re[freq:]
        return carry

    def update(step, carry):
        logit = logit_scr[...]
        mask_soft = jax.nn.sigmoid(logit)
        upper = dot(b_ref[...], mask_soft.astype(bf16))
        cross = mm3(upper, t1c) / norm_area
        swapped = pltpu.roll(cross, lane // 2, 1)
        spec_re = cross[:freq] - swapped[freq:]
        spec_im = -(swapped[:freq] + cross[freq:])
        sre = jnp.concatenate([spec_re] * kernels, axis=0)
        sim = jnp.concatenate([spec_im] * kernels, axis=0)
        pre = pre_ref[...]
        pim = pim_ref[...]
        amp_re = pre * sre - pim * sim
        amp_im = pre * sim + pim * sre
        waves = mm3(amp_re + pltpu.roll(amp_im, lane // 2, 1), wvc)
        wre_scr[...] = waves[:, :side].astype(bf16)
        wim_scr[...] = waves[:, side:].astype(bf16)
        inten_scr[...] = jnp.zeros_like(inten_scr)
        lax.fori_loop(0, kernels, forward, 0, unroll=6)
        resist = jax.nn.sigmoid(resist_slope * (inten_scr[...] - resist_level))
        comb = comb_scr[...]
        target_on = (comb > 0).astype(f32)
        weight_abs = jnp.abs(comb)
        error_term = 2.0 * resist_slope * weight_abs * (resist - target_on) * resist * (1.0 - resist)
        err_scr[...] = 2.0 * error_term
        lax.fori_loop(0, kernels, backward, 0, unroll=6)
        damp = mm3(dcat_scr[...], t2c)
        damp_sw = pltpu.roll(damp, lane // 2, 1)
        t_re = pre * damp + pim * damp_sw
        t_im = pre * damp_sw - pim * damp
        dspec_re = t_re[:freq]
        dspec_im = t_im[:freq]
        for i in range(1, kernels):
            dspec_re = dspec_re + t_re[i * freq:(i + 1) * freq]
            dspec_im = dspec_im + t_im[i * freq:(i + 1) * freq]
        dcross = jnp.concatenate(
            [
                dspec_re + pltpu.roll(-dspec_im, lane // 2, 1),
                -dspec_im + pltpu.roll(-dspec_re, lane // 2, 1),
            ],
            axis=0,
        )
        dupper = mm3(dcross, t3c) / norm_area
        dmask = dot(bt_ref[...], dupper.astype(bf16))
        grad_logit = dmask * mask_soft * (1.0 - mask_soft)
        step_scale = lax.rsqrt(jnp.mean(grad_logit * grad_logit) + 1e-06)
        logit_scr[...] = logit - step_rate * step_scale * grad_logit
        return carry

    lax.fori_loop(0, steps_ref[pl.program_id(0)], update, 0)
    out_ref[...] = logit_scr[MARGIN:MARGIN + CORE, MARGIN:MARGIN + CORE]


def lane_pad(x, width):
    return np.pad(x, ((0, 0), (0, width - x.shape[1])))


def row_pad(x, height):
    return np.pad(x, ((0, height - x.shape[0]), (0, 0)))


def spectral_constants(side_len, freq_count, lane):
    freq_values = np.arange(freq_count, dtype=np.int64) - freq_count // 2
    pixel_pos = np.arange(side_len, dtype=np.int64)
    phase_idx = np.mod(freq_values[:, None] * pixel_pos[None, :], side_len)
    angles = phase_idx.astype(np.float32) * np.float32(2.0 * math.pi / side_len)
    cos_tab = np.cos(angles.astype(np.float64)).astype(np.float32)
    sin_tab = np.sin(angles.astype(np.float64)).astype(np.float32)
    cos_t = cos_tab.T
    sin_t = sin_tab.T
    half = lane // 2
    t1 = np.concatenate([lane_pad(cos_t, half), lane_pad(sin_t, half)], axis=1)
    wv = np.concatenate(
        [
            row_pad(np.concatenate([cos_tab, sin_tab], axis=1), half),
            row_pad(np.concatenate([-sin_tab, cos_tab], axis=1), half),
        ],
        axis=0,
    )
    t2 = np.concatenate(
        [
            np.concatenate([lane_pad(cos_t, half), lane_pad(-sin_t, half)], axis=1),
            np.concatenate([lane_pad(sin_t, half), lane_pad(cos_t, half)], axis=1),
        ],
        axis=0,
    )
    t3 = np.concatenate([row_pad(cos_tab, half), row_pad(sin_tab, half)], axis=0)
    basis_full = np.concatenate([cos_tab, sin_tab], axis=0)
    return basis_full, [t1, wv, t2, t3]


def tiles_call(steps, kernel_weight, logit_parts, comb_parts, pupil_spectra):
    rows, width = logit_parts[1].shape
    kernels = pupil_spectra.shape[1]
    freq, side, lane = KF, TILE, 128
    basis_full, tables = spectral_constants(side, freq, lane)
    basis_bf = jnp.asarray(basis_full).astype(jnp.bfloat16)
    tables = [jnp.asarray(t) for t in tables]
    pupil = pupil_spectra.reshape(2, kernels * freq, freq)
    consts = [pupil, basis_bf.T, basis_bf] + tables
    smem = pl.BlockSpec(memory_space=pltpu.MemorySpace.SMEM)
    ext_spec = pl.BlockSpec((rows, width), lambda t: (0, 0))
    const_specs = [pl.BlockSpec(c.shape, lambda t, n=c.ndim: (0,) * n) for c in consts]
    split_scratch = []
    for table in tables:
        split_scratch.append(pltpu.VMEM((3 * table.shape[0], table.shape[1]), jnp.bfloat16))
    return pl.pallas_call(
        tile_kernel,
        grid=(width // CORE,),
        out_shape=jax.ShapeDtypeStruct((CORE, width), jnp.float32),
        in_specs=[smem, smem] + [ext_spec] * 6 + const_specs,
        out_specs=pl.BlockSpec((CORE, CORE), lambda t: (0, t)),
        scratch_shapes=[
            pltpu.VMEM((side, side), jnp.float32),
            pltpu.VMEM((side, side), jnp.float32),
            pltpu.VMEM((kernels * freq, lane), jnp.float32),
            pltpu.VMEM((kernels * freq, lane), jnp.float32),
        ]
        + split_scratch
        + [
            pltpu.VMEM((kernels * freq, side), jnp.bfloat16),
            pltpu.VMEM((kernels * freq, side), jnp.bfloat16),
            pltpu.VMEM((kernels, 2, side, side), jnp.float32),
            pltpu.VMEM((side, side), jnp.float32),
            pltpu.VMEM((side, side), jnp.float32),
            pltpu.VMEM((kernels * freq, 2 * side), jnp.float32),
        ],
        compiler_params=pltpu.CompilerParams(vmem_limit_bytes=56 * 1024 * 1024),
    )(steps, kernel_weight, *logit_parts, *comb_parts, *consts)


def on_device(mask_logit, target, pixel_weight, tile_steps, pupil_spectra, kernel_weight):
    combined = jnp.where(target == 1, pixel_weight, -pixel_weight)
    state_field = mask_logit
    comb_parts = None
    for round_index in range(ROUNDS):
        if comb_parts is None:
            before, after = halo_parts(jnp.stack([state_field, combined]), "row", 1, MARGIN)
            logit_parts = (before[0], state_field, after[0])
            comb_parts = (before[1], combined, after[1])
        else:
            before, after = halo_parts(state_field, "row", 0, MARGIN)
            logit_parts = (before, state_field, after)
        own_steps = tile_steps[round_index, 0]
        state_field = tiles_call(own_steps, kernel_weight, logit_parts, comb_parts, pupil_spectra)
    return state_field


def solution(mesh):
    return jax.shard_map(
        on_device,
        mesh=mesh,
        in_specs=(
            P(("grp", "row"), None),
            P(("grp", "row"), None),
            P(("grp", "row"), None),
            P(None, ("grp", "row"), None),
            P(),
            P(),
        ),
        out_specs=P(("grp", "row"), None),
        check_vma=False,
    )
```

```python
import math

import jax
import numpy as np
import jax.numpy as jnp
from jax import lax
from jax.experimental import pallas as pl
from jax.experimental.pallas import tpu as pltpu
from jax.sharding import PartitionSpec as P

CORE = 128
MARGIN = 128
KF = 32
ROUNDS = 2
TILE = 384


resist_slope = 4.0
resist_level = 1.0
step_rate = 0.1


def halo_parts(shard, axis, dim, width):
    size, length = (lax.axis_size(axis), shard.shape[dim])
    up = [(i, (i + 1) % size) for i in range(size - 1)]
    down = [(j, i) for i, j in up]
    last = lax.slice_in_dim(shard, length - width, length, axis=dim)
    first = lax.slice_in_dim(shard, 0, width, axis=dim)
    return lax.ppermute(last, axis, up), lax.ppermute(first, axis, down)


def extended_2(shard, sides, width):
    for axis, dim in sides:
        size, length = (lax.axis_size(axis), shard.shape[dim])
        up = [(i, (i + 1) % size) for i in range(size - 1)]
        down = [(j, i) for i, j in up]
        last = lax.slice_in_dim(shard, length - width, length, axis=dim)
        first = lax.slice_in_dim(shard, 0, width, axis=dim)
        before = lax.ppermute(last, axis, up)
        after = lax.ppermute(first, axis, down)
        shard = jnp.concatenate([before, shard, after], axis=dim)
    return shard


def spectral_tables(side_len, freq_count):
    freq_values = jnp.arange(freq_count, dtype=jnp.int32) - freq_count // 2
    pixel_pos = jnp.arange(side_len, dtype=jnp.int32)
    phase_idx = jnp.mod(freq_values[:, None] * pixel_pos[None, :], side_len)
    angles = phase_idx.astype(jnp.float32) * (2.0 * math.pi / side_len)
    return (jnp.cos(angles), jnp.sin(angles))


def split_bf(x):
    hi = x.astype(jnp.bfloat16)
    lo = (x - hi.astype(jnp.float32)).astype(jnp.bfloat16)
    return hi, lo


def tile_kernel(
    steps_ref, w_ref, lb_ref, lo_ref, la_ref, cb_ref, co_ref, ca_ref, pupil_ref, bt_ref, b_ref, t1_ref, wv_ref, t2_ref,
    t3_ref, out_ref, logit_scr, comb_scr, pre_ref, pim_ref, t1c, wvc, t2c, t3c, wre_scr, wim_scr,
    field_scr, inten_scr, err_scr, dcat_scr,
):
    kernels = field_scr.shape[0]
    side = field_scr.shape[2]
    freq = wre_scr.shape[0] // kernels
    lane = pre_ref.shape[1]
    norm_area = float(side * side)
    f32 = jnp.float32
    bf16 = jnp.bfloat16

    def dot(a, b):
        return jnp.dot(a, b, preferred_element_type=f32)

    for table, cat_ref in ((t1_ref, t1c), (wv_ref, wvc), (t2_ref, t2c), (t3_ref, t3c)):
        hi, lo = split_bf(table[...])
        depth = table.shape[0]
        cat_ref[:depth] = hi
        cat_ref[depth:2 * depth] = hi
        cat_ref[2 * depth:] = lo

    def mm3(x, cat_ref):
        x_hi, x_lo = split_bf(x)
        return dot(jnp.concatenate([x_hi, x_lo, x_hi], axis=1), cat_ref[...])

    tile = pl.program_id(0)
    width = lo_ref.shape[1]
    band = lo_ref.shape[0]
    for column in range(width // CORE):

        @pl.when(tile == column)
        def _():
            start = column * CORE - MARGIN
            src_lo = max(start, 0)
            src_hi = min(start + side, width)
            parts = ((logit_scr, (lb_ref, lo_ref, la_ref), 0), (comb_scr, (cb_ref, co_ref, ca_ref), 1))
            for dst, srcs, which in parts:
                if src_lo > start:
                    dst[:, : src_lo - start] = jnp.zeros((side, src_lo - start), f32)
                if src_hi < start + side:
                    dst[:, src_hi - start :] = jnp.zeros((side, start + side - src_hi), f32)
                for index, src in enumerate(srcs):
                    lead = (which,) if len(src.shape) == 3 else ()
                    dst[index * band : (index + 1) * band, src_lo - start : src_hi - start] = src[
                        lead + (slice(None), slice(src_lo, src_hi))
                    ]

    for pad_ref, part in ((pre_ref, 0), (pim_ref, 1)):
        pad_ref[...] = jnp.zeros_like(pad_ref)
        pad_ref[:, :freq] = pupil_ref[part]

    def forward(k, carry):
        r0 = pl.multiple_of(k * freq, freq)
        a0 = wre_scr[pl.ds(r0, freq), :]
        a1 = wim_scr[pl.ds(r0, freq), :]
        c0 = jnp.concatenate([a0, -a1], axis=0)
        c1 = jnp.concatenate([a1, a0], axis=0)
        basis_t = bt_ref[...]
        f_re = dot(basis_t, c0).astype(bf16).astype(f32)
        f_im = dot(basis_t, c1).astype(bf16).astype(f32)
        field_scr[k, 0] = f_re
        field_scr[k, 1] = f_im
        inten_scr[...] += w_ref[k] * (f_re * f_re + f_im * f_im)
        return carry

    def backward(k, carry):
        scale = w_ref[k] * err_scr[...]
        basis = b_ref[...]
        g_re = (scale * field_scr[k, 0]).astype(bf16)
        g_im = (scale * field_scr[k, 1]).astype(bf16)
        p_re = dot(basis, g_re)
        p_im = dot(basis, g_im)
        r0 = pl.multiple_of(k * freq, freq)
        dcat_scr[pl.ds(r0, freq), :side] = p_re[:freq] + p_im[freq:]
        dcat_scr[pl.ds(r0, freq), side:] = p_im[:freq] - p_re[freq:]
        return carry

    def update(step, carry):
        logit = logit_scr[...]
        mask_soft = jax.nn.sigmoid(logit)
        upper = dot(b_ref[...], mask_soft.astype(bf16))
        cross = mm3(upper, t1c) / norm_area
        swapped = pltpu.roll(cross, lane // 2, 1)
        spec_re = cross[:freq] - swapped[freq:]
        spec_im = -(swapped[:freq] + cross[freq:])
        sre = jnp.concatenate([spec_re] * kernels, axis=0)
        sim = jnp.concatenate([spec_im] * kernels, axis=0)
        pre = pre_ref[...]
        pim = pim_ref[...]
        amp_re = pre * sre - pim * sim
        amp_im = pre * sim + pim * sre
        waves = mm3(amp_re + pltpu.roll(amp_im, lane // 2, 1), wvc)
        wre_scr[...] = waves[:, :side].astype(bf16)
        wim_scr[...] = waves[:, side:].astype(bf16)
        inten_scr[...] = jnp.zeros_like(inten_scr)
        lax.fori_loop(0, kernels, forward, 0, unroll=6)
        resist = jax.nn.sigmoid(resist_slope * (inten_scr[...] - resist_level))
        comb = comb_scr[...]
        target_on = (comb > 0).astype(f32)
        weight_abs = jnp.abs(comb)
        error_term = 2.0 * resist_slope * weight_abs * (resist - target_on) * resist * (1.0 - resist)
        err_scr[...] = 2.0 * error_term
        lax.fori_loop(0, kernels, backward, 0, unroll=6)
        damp = mm3(dcat_scr[...], t2c)
        damp_sw = pltpu.roll(damp, lane // 2, 1)
        t_re = pre * damp + pim * damp_sw
        t_im = pre * damp_sw - pim * damp
        dspec_re = t_re[:freq]
        dspec_im = t_im[:freq]
        for i in range(1, kernels):
            dspec_re = dspec_re + t_re[i * freq:(i + 1) * freq]
            dspec_im = dspec_im + t_im[i * freq:(i + 1) * freq]
        dcross = jnp.concatenate(
            [
                dspec_re + pltpu.roll(-dspec_im, lane // 2, 1),
                -dspec_im + pltpu.roll(-dspec_re, lane // 2, 1),
            ],
            axis=0,
        )
        dupper = mm3(dcross, t3c) / norm_area
        dmask = dot(bt_ref[...], dupper.astype(bf16))
        grad_logit = dmask * mask_soft * (1.0 - mask_soft)
        step_scale = lax.rsqrt(jnp.mean(grad_logit * grad_logit) + 1e-06)
        logit_scr[...] = logit - step_rate * step_scale * grad_logit
        return carry

    lax.fori_loop(0, steps_ref[pl.program_id(0)], update, 0)
    out_ref[...] = logit_scr[MARGIN:MARGIN + CORE, MARGIN:MARGIN + CORE]


def lane_pad(x, width):
    return np.pad(x, ((0, 0), (0, width - x.shape[1])))


def row_pad(x, height):
    return np.pad(x, ((0, height - x.shape[0]), (0, 0)))


def spectral_constants(side_len, freq_count, lane):
    freq_values = np.arange(freq_count, dtype=np.int64) - freq_count // 2
    pixel_pos = np.arange(side_len, dtype=np.int64)
    phase_idx = np.mod(freq_values[:, None] * pixel_pos[None, :], side_len)
    angles = phase_idx.astype(np.float32) * np.float32(2.0 * math.pi / side_len)
    cos_tab = np.cos(angles.astype(np.float64)).astype(np.float32)
    sin_tab = np.sin(angles.astype(np.float64)).astype(np.float32)
    cos_t = cos_tab.T
    sin_t = sin_tab.T
    half = lane // 2
    t1 = np.concatenate([lane_pad(cos_t, half), lane_pad(sin_t, half)], axis=1)
    wv = np.concatenate(
        [
            row_pad(np.concatenate([cos_tab, sin_tab], axis=1), half),
            row_pad(np.concatenate([-sin_tab, cos_tab], axis=1), half),
        ],
        axis=0,
    )
    t2 = np.concatenate(
        [
            np.concatenate([lane_pad(cos_t, half), lane_pad(-sin_t, half)], axis=1),
            np.concatenate([lane_pad(sin_t, half), lane_pad(cos_t, half)], axis=1),
        ],
        axis=0,
    )
    t3 = np.concatenate([row_pad(cos_tab, half), row_pad(sin_tab, half)], axis=0)
    basis_full = np.concatenate([cos_tab, sin_tab], axis=0)
    return basis_full, [t1, wv, t2, t3]


def tiles_call(steps, kernel_weight, logit_parts, comb_parts, pupil_spectra):
    rows, width = logit_parts[1].shape
    parts = list(logit_parts) + list(comb_parts)
    part_specs = [pl.BlockSpec(p.shape, lambda t, n=p.ndim: (0,) * n) for p in parts]
    kernels = pupil_spectra.shape[1]
    freq, side, lane = KF, TILE, 128
    basis_full, tables = spectral_constants(side, freq, lane)
    basis_bf = jnp.asarray(basis_full).astype(jnp.bfloat16)
    tables = [jnp.asarray(t) for t in tables]
    pupil = pupil_spectra.reshape(2, kernels * freq, freq)
    consts = [pupil, basis_bf.T, basis_bf] + tables
    smem = pl.BlockSpec(memory_space=pltpu.MemorySpace.SMEM)
    ext_spec = pl.BlockSpec((rows, width), lambda t: (0, 0))
    const_specs = [pl.BlockSpec(c.shape, lambda t, n=c.ndim: (0,) * n) for c in consts]
    split_scratch = []
    for table in tables:
        split_scratch.append(pltpu.VMEM((3 * table.shape[0], table.shape[1]), jnp.bfloat16))
    return pl.pallas_call(
        tile_kernel,
        grid=(width // CORE,),
        out_shape=jax.ShapeDtypeStruct((CORE, width), jnp.float32),
        in_specs=[smem, smem] + part_specs + const_specs,
        out_specs=pl.BlockSpec((CORE, CORE), lambda t: (0, t)),
        scratch_shapes=[
            pltpu.VMEM((side, side), jnp.float32),
            pltpu.VMEM((side, side), jnp.float32),
            pltpu.VMEM((kernels * freq, lane), jnp.float32),
            pltpu.VMEM((kernels * freq, lane), jnp.float32),
        ]
        + split_scratch
        + [
            pltpu.VMEM((kernels * freq, side), jnp.bfloat16),
            pltpu.VMEM((kernels * freq, side), jnp.bfloat16),
            pltpu.VMEM((kernels, 2, side, side), jnp.float32),
            pltpu.VMEM((side, side), jnp.float32),
            pltpu.VMEM((side, side), jnp.float32),
            pltpu.VMEM((kernels * freq, 2 * side), jnp.float32),
        ],
        compiler_params=pltpu.CompilerParams(vmem_limit_bytes=56 * 1024 * 1024),
    )(steps, kernel_weight, *parts, *consts)


def on_device(mask_logit, target, pixel_weight, tile_steps, pupil_spectra, kernel_weight):
    combined = jnp.where(target == 1, pixel_weight, -pixel_weight)
    state_field = mask_logit
    comb_parts = None
    for round_index in range(ROUNDS):
        if comb_parts is None:
            before, after = halo_parts(jnp.stack([state_field, combined]), "row", 1, MARGIN)
            logit_parts = (before, state_field, after)
            comb_parts = (before, combined, after)
        else:
            before, after = halo_parts(state_field[None], "row", 1, MARGIN)
            logit_parts = (before, state_field, after)
        own_steps = tile_steps[round_index, 0]
        state_field = tiles_call(own_steps, kernel_weight, logit_parts, comb_parts, pupil_spectra)
    return state_field


def solution(mesh):
    return jax.shard_map(
        on_device,
        mesh=mesh,
        in_specs=(
            P(("grp", "row"), None),
            P(("grp", "row"), None),
            P(("grp", "row"), None),
            P(None, ("grp", "row"), None),
            P(),
            P(),
        ),
        out_specs=P(("grp", "row"), None),
        check_vma=False,
    )
```

```python
import math

import jax
import numpy as np
import jax.numpy as jnp
from jax import lax
from jax.experimental import pallas as pl
from jax.experimental.pallas import tpu as pltpu
from jax.sharding import PartitionSpec as P

CORE = 128
MARGIN = 128
KF = 32
ROUNDS = 2
TILE = 384


resist_slope = 4.0
resist_level = 1.0
step_rate = 0.1


def halo_parts(shard, axis, dim, width):
    size, length = (lax.axis_size(axis), shard.shape[dim])
    up = [(i, (i + 1) % size) for i in range(size - 1)]
    down = [(j, i) for i, j in up]
    last = lax.slice_in_dim(shard, length - width, length, axis=dim)
    first = lax.slice_in_dim(shard, 0, width, axis=dim)
    return lax.ppermute(last, axis, up), lax.ppermute(first, axis, down)


def extended_2(shard, sides, width):
    for axis, dim in sides:
        size, length = (lax.axis_size(axis), shard.shape[dim])
        up = [(i, (i + 1) % size) for i in range(size - 1)]
        down = [(j, i) for i, j in up]
        last = lax.slice_in_dim(shard, length - width, length, axis=dim)
        first = lax.slice_in_dim(shard, 0, width, axis=dim)
        before = lax.ppermute(last, axis, up)
        after = lax.ppermute(first, axis, down)
        shard = jnp.concatenate([before, shard, after], axis=dim)
    return shard


def spectral_tables(side_len, freq_count):
    freq_values = jnp.arange(freq_count, dtype=jnp.int32) - freq_count // 2
    pixel_pos = jnp.arange(side_len, dtype=jnp.int32)
    phase_idx = jnp.mod(freq_values[:, None] * pixel_pos[None, :], side_len)
    angles = phase_idx.astype(jnp.float32) * (2.0 * math.pi / side_len)
    return (jnp.cos(angles), jnp.sin(angles))


def split_bf(x):
    hi = x.astype(jnp.bfloat16)
    lo = (x - hi.astype(jnp.float32)).astype(jnp.bfloat16)
    return hi, lo


def tile_kernel(
    steps_ref, w_ref, lb_ref, lo_ref, la_ref, cb_ref, co_ref, ca_ref, pupil_ref, bt_ref, b_ref, t1c, wvc, t2c,
    t3c, out_ref, logit_scr, comb_scr, pre_ref, pim_ref, wre_scr, wim_scr,
    field_scr, inten_scr, err_scr, dcat_scr,
):
    kernels = field_scr.shape[0]
    side = field_scr.shape[2]
    freq = wre_scr.shape[0] // kernels
    lane = pre_ref.shape[1]
    norm_area = float(side * side)
    f32 = jnp.float32
    bf16 = jnp.bfloat16

    def dot(a, b):
        return jnp.dot(a, b, preferred_element_type=f32)

    def mm3(x, cat_ref):
        x_hi, x_lo = split_bf(x)
        return dot(jnp.concatenate([x_hi, x_lo, x_hi], axis=1), cat_ref[...])

    tile = pl.program_id(0)
    width = lo_ref.shape[1]
    band = lo_ref.shape[0]
    for column in range(width // CORE):

        @pl.when(tile == column)
        def _():
            start = column * CORE - MARGIN
            src_lo = max(start, 0)
            src_hi = min(start + side, width)
            parts = ((logit_scr, (lb_ref, lo_ref, la_ref), 0), (comb_scr, (cb_ref, co_ref, ca_ref), 1))
            for dst, srcs, which in parts:
                if src_lo > start:
                    dst[:, : src_lo - start] = jnp.zeros((side, src_lo - start), f32)
                if src_hi < start + side:
                    dst[:, src_hi - start :] = jnp.zeros((side, start + side - src_hi), f32)
                for index, src in enumerate(srcs):
                    lead = (which,) if len(src.shape) == 3 else ()
                    dst[index * band : (index + 1) * band, src_lo - start : src_hi - start] = src[
                        lead + (slice(None), slice(src_lo, src_hi))
                    ]

    for pad_ref, part in ((pre_ref, 0), (pim_ref, 1)):
        pad_ref[...] = jnp.zeros_like(pad_ref)
        pad_ref[:, :freq] = pupil_ref[part]

    def forward(k, carry):
        r0 = pl.multiple_of(k * freq, freq)
        a0 = wre_scr[pl.ds(r0, freq), :]
        a1 = wim_scr[pl.ds(r0, freq), :]
        c0 = jnp.concatenate([a0, -a1], axis=0)
        c1 = jnp.concatenate([a1, a0], axis=0)
        basis_t = bt_ref[...]
        f_re = dot(basis_t, c0).astype(bf16).astype(f32)
        f_im = dot(basis_t, c1).astype(bf16).astype(f32)
        field_scr[k, 0] = f_re
        field_scr[k, 1] = f_im
        inten_scr[...] += w_ref[k] * (f_re * f_re + f_im * f_im)
        return carry

    def backward(k, carry):
        scale = w_ref[k] * err_scr[...]
        basis = b_ref[...]
        g_re = (scale * field_scr[k, 0]).astype(bf16)
        g_im = (scale * field_scr[k, 1]).astype(bf16)
        p_re = dot(basis, g_re)
        p_im = dot(basis, g_im)
        r0 = pl.multiple_of(k * freq, freq)
        dcat_scr[pl.ds(r0, freq), :side] = p_re[:freq] + p_im[freq:]
        dcat_scr[pl.ds(r0, freq), side:] = p_im[:freq] - p_re[freq:]
        return carry

    def update(step, carry):
        logit = logit_scr[...]
        mask_soft = jax.nn.sigmoid(logit)
        upper = dot(b_ref[...], mask_soft.astype(bf16))
        cross = mm3(upper, t1c) / norm_area
        swapped = pltpu.roll(cross, lane // 2, 1)
        spec_re = cross[:freq] - swapped[freq:]
        spec_im = -(swapped[:freq] + cross[freq:])
        sre = jnp.concatenate([spec_re] * kernels, axis=0)
        sim = jnp.concatenate([spec_im] * kernels, axis=0)
        pre = pre_ref[...]
        pim = pim_ref[...]
        amp_re = pre * sre - pim * sim
        amp_im = pre * sim + pim * sre
        waves = mm3(amp_re + pltpu.roll(amp_im, lane // 2, 1), wvc)
        wre_scr[...] = waves[:, :side].astype(bf16)
        wim_scr[...] = waves[:, side:].astype(bf16)
        inten_scr[...] = jnp.zeros_like(inten_scr)
        lax.fori_loop(0, kernels, forward, 0, unroll=6)
        resist = jax.nn.sigmoid(resist_slope * (inten_scr[...] - resist_level))
        comb = comb_scr[...]
        target_on = (comb > 0).astype(f32)
        weight_abs = jnp.abs(comb)
        error_term = 2.0 * resist_slope * weight_abs * (resist - target_on) * resist * (1.0 - resist)
        err_scr[...] = 2.0 * error_term
        lax.fori_loop(0, kernels, backward, 0, unroll=6)
        damp = mm3(dcat_scr[...], t2c)
        damp_sw = pltpu.roll(damp, lane // 2, 1)
        t_re = pre * damp + pim * damp_sw
        t_im = pre * damp_sw - pim * damp
        dspec_re = t_re[:freq]
        dspec_im = t_im[:freq]
        for i in range(1, kernels):
            dspec_re = dspec_re + t_re[i * freq:(i + 1) * freq]
            dspec_im = dspec_im + t_im[i * freq:(i + 1) * freq]
        dcross = jnp.concatenate(
            [
                dspec_re + pltpu.roll(-dspec_im, lane // 2, 1),
                -dspec_im + pltpu.roll(-dspec_re, lane // 2, 1),
            ],
            axis=0,
        )
        dupper = mm3(dcross, t3c) / norm_area
        dmask = dot(bt_ref[...], dupper.astype(bf16))
        grad_logit = dmask * mask_soft * (1.0 - mask_soft)
        step_scale = lax.rsqrt(jnp.mean(grad_logit * grad_logit) + 1e-06)
        logit_scr[...] = logit - step_rate * step_scale * grad_logit
        return carry

    lax.fori_loop(0, steps_ref[pl.program_id(0)], update, 0)
    out_ref[...] = logit_scr[MARGIN:MARGIN + CORE, MARGIN:MARGIN + CORE]


def lane_pad(x, width):
    return np.pad(x, ((0, 0), (0, width - x.shape[1])))


def row_pad(x, height):
    return np.pad(x, ((0, height - x.shape[0]), (0, 0)))


def spectral_constants(side_len, freq_count, lane):
    freq_values = np.arange(freq_count, dtype=np.int64) - freq_count // 2
    pixel_pos = np.arange(side_len, dtype=np.int64)
    phase_idx = np.mod(freq_values[:, None] * pixel_pos[None, :], side_len)
    angles = phase_idx.astype(np.float32) * np.float32(2.0 * math.pi / side_len)
    cos_tab = np.cos(angles.astype(np.float64)).astype(np.float32)
    sin_tab = np.sin(angles.astype(np.float64)).astype(np.float32)
    cos_t = cos_tab.T
    sin_t = sin_tab.T
    half = lane // 2
    t1 = np.concatenate([lane_pad(cos_t, half), lane_pad(sin_t, half)], axis=1)
    wv = np.concatenate(
        [
            row_pad(np.concatenate([cos_tab, sin_tab], axis=1), half),
            row_pad(np.concatenate([-sin_tab, cos_tab], axis=1), half),
        ],
        axis=0,
    )
    t2 = np.concatenate(
        [
            np.concatenate([lane_pad(cos_t, half), lane_pad(-sin_t, half)], axis=1),
            np.concatenate([lane_pad(sin_t, half), lane_pad(cos_t, half)], axis=1),
        ],
        axis=0,
    )
    t3 = np.concatenate([row_pad(cos_tab, half), row_pad(sin_tab, half)], axis=0)
    basis_full = np.concatenate([cos_tab, sin_tab], axis=0)
    return basis_full, [t1, wv, t2, t3]


def split_table(table):
    hi = table.astype(jnp.bfloat16)
    lo = (table - hi.astype(np.float32)).astype(jnp.bfloat16)
    return np.concatenate([hi, hi, lo], axis=0)


def tiles_call(steps, kernel_weight, logit_parts, comb_parts, pupil_spectra):
    rows, width = logit_parts[1].shape
    parts = list(logit_parts) + list(comb_parts)
    vmem_whole = pl.BlockSpec(memory_space=pltpu.MemorySpace.VMEM)
    part_specs = [vmem_whole] * len(parts)
    kernels = pupil_spectra.shape[1]
    freq, side, lane = KF, TILE, 128
    basis_full, tables = spectral_constants(side, freq, lane)
    basis_bf = jnp.asarray(basis_full).astype(jnp.bfloat16)
    tables = [jnp.asarray(split_table(t)) for t in tables]
    pupil = pupil_spectra.reshape(2, kernels * freq, freq)
    consts = [pupil, basis_bf.T, basis_bf] + tables
    smem = pl.BlockSpec(memory_space=pltpu.MemorySpace.SMEM)
    ext_spec = pl.BlockSpec((rows, width), lambda t: (0, 0))
    const_specs = [vmem_whole] * len(consts)
    return pl.pallas_call(
        tile_kernel,
        grid=(width // CORE,),
        out_shape=jax.ShapeDtypeStruct((CORE, width), jnp.float32),
        in_specs=[smem, smem] + part_specs + const_specs,
        out_specs=pl.BlockSpec((CORE, CORE), lambda t: (0, t)),
        scratch_shapes=[
            pltpu.VMEM((side, side), jnp.float32),
            pltpu.VMEM((side, side), jnp.float32),
            pltpu.VMEM((kernels * freq, lane), jnp.float32),
            pltpu.VMEM((kernels * freq, lane), jnp.float32),
        ]
        + [
            pltpu.VMEM((kernels * freq, side), jnp.bfloat16),
            pltpu.VMEM((kernels * freq, side), jnp.bfloat16),
            pltpu.VMEM((kernels, 2, side, side), jnp.float32),
            pltpu.VMEM((side, side), jnp.float32),
            pltpu.VMEM((side, side), jnp.float32),
            pltpu.VMEM((kernels * freq, 2 * side), jnp.float32),
        ],
        compiler_params=pltpu.CompilerParams(vmem_limit_bytes=56 * 1024 * 1024),
    )(steps, kernel_weight, *parts, *consts)


def on_device(mask_logit, target, pixel_weight, tile_steps, pupil_spectra, kernel_weight):
    combined = jnp.where(target == 1, pixel_weight, -pixel_weight)
    state_field = mask_logit
    comb_parts = None
    for round_index in range(ROUNDS):
        if comb_parts is None:
            before, after = halo_parts(jnp.stack([state_field, combined]), "row", 1, MARGIN)
            logit_parts = (before, state_field, after)
            comb_parts = (before, combined, after)
        else:
            before, after = halo_parts(state_field[None], "row", 1, MARGIN)
            logit_parts = (before, state_field, after)
        own_steps = tile_steps[round_index, 0]
        state_field = tiles_call(own_steps, kernel_weight, logit_parts, comb_parts, pupil_spectra)
    return state_field


def solution(mesh):
    return jax.shard_map(
        on_device,
        mesh=mesh,
        in_specs=(
            P(("grp", "row"), None),
            P(("grp", "row"), None),
            P(("grp", "row"), None),
            P(None, ("grp", "row"), None),
            P(),
            P(),
        ),
        out_specs=P(("grp", "row"), None),
        check_vma=False,
    )
```

```python
import math

import jax
import numpy as np
import jax.numpy as jnp
from jax import lax
from jax.experimental import pallas as pl
from jax.experimental.pallas import tpu as pltpu
from jax.sharding import PartitionSpec as P

CORE = 128
MARGIN = 128
KF = 32
ROUNDS = 2
TILE = 384


resist_slope = 4.0
resist_level = 1.0
step_rate = 0.1


def halo_parts(shard, axis, dim, width):
    size, length = (lax.axis_size(axis), shard.shape[dim])
    up = [(i, (i + 1) % size) for i in range(size - 1)]
    down = [(j, i) for i, j in up]
    last = lax.slice_in_dim(shard, length - width, length, axis=dim)
    first = lax.slice_in_dim(shard, 0, width, axis=dim)
    return lax.ppermute(last, axis, up), lax.ppermute(first, axis, down)


def extended_2(shard, sides, width):
    for axis, dim in sides:
        size, length = (lax.axis_size(axis), shard.shape[dim])
        up = [(i, (i + 1) % size) for i in range(size - 1)]
        down = [(j, i) for i, j in up]
        last = lax.slice_in_dim(shard, length - width, length, axis=dim)
        first = lax.slice_in_dim(shard, 0, width, axis=dim)
        before = lax.ppermute(last, axis, up)
        after = lax.ppermute(first, axis, down)
        shard = jnp.concatenate([before, shard, after], axis=dim)
    return shard


def spectral_tables(side_len, freq_count):
    freq_values = jnp.arange(freq_count, dtype=jnp.int32) - freq_count // 2
    pixel_pos = jnp.arange(side_len, dtype=jnp.int32)
    phase_idx = jnp.mod(freq_values[:, None] * pixel_pos[None, :], side_len)
    angles = phase_idx.astype(jnp.float32) * (2.0 * math.pi / side_len)
    return (jnp.cos(angles), jnp.sin(angles))


def split_bf(x):
    hi = x.astype(jnp.bfloat16)
    lo = (x - hi.astype(jnp.float32)).astype(jnp.bfloat16)
    return hi, lo


def tile_kernel(
    steps_ref, w_ref, lb_ref, lo_ref, la_ref, cb_ref, co_ref, ca_ref, pupil_ref, bt_ref, b_ref, t1c, wvc, t2c,
    t3c, out_ref, logit_scr, comb_scr, pre_ref, pim_ref, wre_scr, wim_scr,
    field_scr, inten_scr, err_scr, dcat_scr, ton_scr,
):
    kernels = field_scr.shape[0]
    side = field_scr.shape[2]
    freq = wre_scr.shape[0] // kernels
    lane = pre_ref.shape[1]
    norm_area = float(side * side)
    f32 = jnp.float32
    bf16 = jnp.bfloat16

    def dot(a, b):
        return jnp.dot(a, b, preferred_element_type=f32)

    def mm3(x, cat_ref):
        x_hi, x_lo = split_bf(x)
        return dot(jnp.concatenate([x_hi, x_lo, x_hi], axis=1), cat_ref[...])

    tile = pl.program_id(0)
    width = lo_ref.shape[1]
    band = lo_ref.shape[0]
    for column in range(width // CORE):

        @pl.when(tile == column)
        def _():
            start = column * CORE - MARGIN
            src_lo = max(start, 0)
            src_hi = min(start + side, width)
            parts = ((logit_scr, (lb_ref, lo_ref, la_ref), 0), (comb_scr, (cb_ref, co_ref, ca_ref), 1))
            for dst, srcs, which in parts:
                if src_lo > start:
                    dst[:, : src_lo - start] = jnp.zeros((side, src_lo - start), f32)
                if src_hi < start + side:
                    dst[:, src_hi - start :] = jnp.zeros((side, start + side - src_hi), f32)
                for index, src in enumerate(srcs):
                    lead = (which,) if len(src.shape) == 3 else ()
                    dst[index * band : (index + 1) * band, src_lo - start : src_hi - start] = src[
                        lead + (slice(None), slice(src_lo, src_hi))
                    ]

    comb = comb_scr[...]
    ton_scr[...] = (comb > 0).astype(f32)
    comb_scr[...] = (2.0 * 2.0 * resist_slope) * jnp.abs(comb)

    for pad_ref, part in ((pre_ref, 0), (pim_ref, 1)):
        pad_ref[...] = jnp.zeros_like(pad_ref)
        pad_ref[:, :freq] = pupil_ref[part]

    def field_of(k):
        r0 = pl.multiple_of(k * freq, freq)
        a0 = wre_scr[pl.ds(r0, freq), :]
        a1 = wim_scr[pl.ds(r0, freq), :]
        c0 = jnp.concatenate([a0, -a1], axis=0)
        c1 = jnp.concatenate([a1, a0], axis=0)
        basis_t = bt_ref[...]
        f_re = dot(basis_t, c0).astype(bf16).astype(f32)
        f_im = dot(basis_t, c1).astype(bf16).astype(f32)
        field_scr[k, 0] = f_re
        field_scr[k, 1] = f_im
        return w_ref[k] * (f_re * f_re + f_im * f_im)

    def field_pair(j):
        return field_of(2 * j) + field_of(2 * j + 1)

    def forward(j, carry):
        inten_scr[...] += field_pair(j)
        return carry

    def backward(k, carry):
        scale = w_ref[k] * err_scr[...]
        basis = b_ref[...]
        g_re = (scale * field_scr[k, 0]).astype(bf16)
        g_im = (scale * field_scr[k, 1]).astype(bf16)
        p_re = dot(basis, g_re)
        p_im = dot(basis, g_im)
        r0 = pl.multiple_of(k * freq, freq)
        dcat_scr[pl.ds(r0, freq), :side] = p_re[:freq] + p_im[freq:]
        dcat_scr[pl.ds(r0, freq), side:] = p_im[:freq] - p_re[freq:]
        return carry

    def update(step, carry):
        logit = logit_scr[...]
        mask_soft = jax.nn.sigmoid(logit)
        upper = dot(b_ref[...], mask_soft.astype(bf16))
        cross = mm3(upper, t1c) / norm_area
        swapped = pltpu.roll(cross, lane // 2, 1)
        spec_re = cross[:freq] - swapped[freq:]
        spec_im = -(swapped[:freq] + cross[freq:])
        sre = jnp.concatenate([spec_re] * kernels, axis=0)
        sim = jnp.concatenate([spec_im] * kernels, axis=0)
        pre = pre_ref[...]
        pim = pim_ref[...]
        amp_re = pre * sre - pim * sim
        amp_im = pre * sim + pim * sre
        waves = mm3(amp_re + pltpu.roll(amp_im, lane // 2, 1), wvc)
        wre_scr[...] = waves[:, :side].astype(bf16)
        wim_scr[...] = waves[:, side:].astype(bf16)
        inten_scr[...] = field_pair(0)
        lax.fori_loop(1, kernels // 2, forward, 0, unroll=5)
        resist = jax.nn.sigmoid(resist_slope * (inten_scr[...] - resist_level))
        err_scr[...] = comb_scr[...] * (resist - ton_scr[...]) * resist * (1.0 - resist)
        lax.fori_loop(0, kernels, backward, 0, unroll=6)
        damp = mm3(dcat_scr[...], t2c)
        damp_sw = pltpu.roll(damp, lane // 2, 1)
        t_re = pre * damp + pim * damp_sw
        t_im = pre * damp_sw - pim * damp
        dspec_re = t_re[:freq]
        dspec_im = t_im[:freq]
        for i in range(1, kernels):
            dspec_re = dspec_re + t_re[i * freq:(i + 1) * freq]
            dspec_im = dspec_im + t_im[i * freq:(i + 1) * freq]
        dcross = jnp.concatenate(
            [
                dspec_re + pltpu.roll(-dspec_im, lane // 2, 1),
                -dspec_im + pltpu.roll(-dspec_re, lane // 2, 1),
            ],
            axis=0,
        )
        dupper = mm3(dcross, t3c) / norm_area
        dmask = dot(bt_ref[...], dupper.astype(bf16))
        grad_logit = dmask * mask_soft * (1.0 - mask_soft)
        step_scale = lax.rsqrt(jnp.mean(grad_logit * grad_logit) + 1e-06)
        logit_scr[...] = logit - step_rate * step_scale * grad_logit
        return carry

    lax.fori_loop(0, steps_ref[pl.program_id(0)], update, 0)
    out_ref[...] = logit_scr[MARGIN:MARGIN + CORE, MARGIN:MARGIN + CORE]


def lane_pad(x, width):
    return np.pad(x, ((0, 0), (0, width - x.shape[1])))


def row_pad(x, height):
    return np.pad(x, ((0, height - x.shape[0]), (0, 0)))


def spectral_constants(side_len, freq_count, lane):
    freq_values = np.arange(freq_count, dtype=np.int64) - freq_count // 2
    pixel_pos = np.arange(side_len, dtype=np.int64)
    phase_idx = np.mod(freq_values[:, None] * pixel_pos[None, :], side_len)
    angles = phase_idx.astype(np.float32) * np.float32(2.0 * math.pi / side_len)
    cos_tab = np.cos(angles.astype(np.float64)).astype(np.float32)
    sin_tab = np.sin(angles.astype(np.float64)).astype(np.float32)
    cos_t = cos_tab.T
    sin_t = sin_tab.T
    half = lane // 2
    t1 = np.concatenate([lane_pad(cos_t, half), lane_pad(sin_t, half)], axis=1)
    wv = np.concatenate(
        [
            row_pad(np.concatenate([cos_tab, sin_tab], axis=1), half),
            row_pad(np.concatenate([-sin_tab, cos_tab], axis=1), half),
        ],
        axis=0,
    )
    t2 = np.concatenate(
        [
            np.concatenate([lane_pad(cos_t, half), lane_pad(-sin_t, half)], axis=1),
            np.concatenate([lane_pad(sin_t, half), lane_pad(cos_t, half)], axis=1),
        ],
        axis=0,
    )
    t3 = np.concatenate([row_pad(cos_tab, half), row_pad(sin_tab, half)], axis=0)
    basis_full = np.concatenate([cos_tab, sin_tab], axis=0)
    return basis_full, [t1, wv, t2, t3]


def split_table(table):
    hi = table.astype(jnp.bfloat16)
    lo = (table - hi.astype(np.float32)).astype(jnp.bfloat16)
    return np.concatenate([hi, hi, lo], axis=0)


def tiles_call(steps, kernel_weight, logit_parts, comb_parts, pupil_spectra):
    rows, width = logit_parts[1].shape
    parts = list(logit_parts) + list(comb_parts)
    vmem_whole = pl.BlockSpec(memory_space=pltpu.MemorySpace.VMEM)
    part_specs = [vmem_whole] * len(parts)
    kernels = pupil_spectra.shape[1]
    freq, side, lane = KF, TILE, 128
    basis_full, tables = spectral_constants(side, freq, lane)
    basis_bf = jnp.asarray(basis_full).astype(jnp.bfloat16)
    tables = [jnp.asarray(split_table(t)) for t in tables]
    pupil = pupil_spectra.reshape(2, kernels * freq, freq)
    consts = [pupil, basis_bf.T, basis_bf] + tables
    smem = pl.BlockSpec(memory_space=pltpu.MemorySpace.SMEM)
    ext_spec = pl.BlockSpec((rows, width), lambda t: (0, 0))
    const_specs = [vmem_whole] * len(consts)
    return pl.pallas_call(
        tile_kernel,
        grid=(width // CORE,),
        out_shape=jax.ShapeDtypeStruct((CORE, width), jnp.float32),
        in_specs=[smem, smem] + part_specs + const_specs,
        out_specs=pl.BlockSpec((CORE, CORE), lambda t: (0, t)),
        scratch_shapes=[
            pltpu.VMEM((side, side), jnp.float32),
            pltpu.VMEM((side, side), jnp.float32),
            pltpu.VMEM((kernels * freq, lane), jnp.float32),
            pltpu.VMEM((kernels * freq, lane), jnp.float32),
        ]
        + [
            pltpu.VMEM((kernels * freq, side), jnp.bfloat16),
            pltpu.VMEM((kernels * freq, side), jnp.bfloat16),
            pltpu.VMEM((kernels, 2, side, side), jnp.float32),
            pltpu.VMEM((side, side), jnp.float32),
            pltpu.VMEM((side, side), jnp.float32),
            pltpu.VMEM((kernels * freq, 2 * side), jnp.float32),
            pltpu.VMEM((side, side), jnp.float32),
        ],
        compiler_params=pltpu.CompilerParams(vmem_limit_bytes=56 * 1024 * 1024),
    )(steps, kernel_weight, *parts, *consts)


def on_device(mask_logit, target, pixel_weight, tile_steps, pupil_spectra, kernel_weight):
    combined = jnp.where(target == 1, pixel_weight, -pixel_weight)
    state_field = mask_logit
    comb_parts = None
    for round_index in range(ROUNDS):
        if comb_parts is None:
            before, after = halo_parts(jnp.stack([state_field, combined]), "row", 1, MARGIN)
            logit_parts = (before, state_field, after)
            comb_parts = (before, combined, after)
        else:
            before, after = halo_parts(state_field[None], "row", 1, MARGIN)
            logit_parts = (before, state_field, after)
        own_steps = tile_steps[round_index, 0]
        state_field = tiles_call(own_steps, kernel_weight, logit_parts, comb_parts, pupil_spectra)
    return state_field


def solution(mesh):
    return jax.shard_map(
        on_device,
        mesh=mesh,
        in_specs=(
            P(("grp", "row"), None),
            P(("grp", "row"), None),
            P(("grp", "row"), None),
            P(None, ("grp", "row"), None),
            P(),
            P(),
        ),
        out_specs=P(("grp", "row"), None),
        check_vma=False,
    )
```
